512 devices in a mesh: chan: 128 (over y, z, core), tm: 4 (over x).
Axes of the slice: x: 4, y: 4, z: 16, core: 2. Of those that a mesh axis runs over, the one named last changes fastest.
Arguments:
- voltages: bfloat16 [512, 128, 2, 1024], P('chan', 'tm'), may hold values from -6 to 6
- filter_taps: float32 [12, 1024], replicated, may hold values from -1.75 to 1.75
- flagged: int32 [256], replicated, may hold values from 0 to 1023, as said below
- owners: int32 [1024], replicated, may hold values from 0 to 511, as said below
Outputs:
- visibilities: float32 [1024, 2, 512, 512], P(('chan', 'tm'))
The draws below stay inside these ranges and needn't reach their ends.
Inputs may be any that keep to these rules, and one draw needn't show every extreme that they name: `flagged`: distinct channel numbers. `owners`: each device owns exactly 2 of the 1024 channels, flagged or not; device d is the one with chan index d // 4 and tm index d % 4.
All inputs are finite; a program needn't handle non-finite values.
Results may differ from the reference program's by a relative error of at most 0.0059.
Values may be sent and summed in bfloat16 or wider, within the bound.
No kernel may reach another device: no remote copies, remote signals or barrier semaphores. Data moves between devices by JAX's collectives and lax.ppermute only.
A program may use at most 64 MiB of HBM per device.

```python
import math
import jax
import jax.numpy as jnp
from jax import lax

INPUTS = 512
NCHAN = 1024
TAPS = 12
SPECTRA = 128
NFLAG = 256
CAP = 2


def draw_flagged(key, part):
    shuffled = jax.random.permutation(jax.random.fold_in(key, 11), NCHAN)
    return shuffled[:NFLAG].astype(jnp.int32)


def draw_owners(key, part):
    shuffled = jax.random.permutation(jax.random.fold_in(key, 23), NCHAN).astype(jnp.int32)
    inverse = jnp.argsort(shuffled, stable=True).astype(jnp.int32)
    return (inverse // CAP).astype(jnp.int32)


def shard_levels(stream_key, shape, split, low, high):
    level = 1.0
    for position, shards_of in split:
        heights = jax.random.uniform(jax.random.fold_in(jax.random.fold_in(stream_key, 6), position), (shards_of,), jnp.float32, low / len(split), high / len(split))
        level = level * jnp.repeat(jnp.exp(heights), shape[position] // shards_of).reshape((-1,) + (1,) * (len(shape) - 1 - position))
    return level


def bell_draw(stream_key, dims, width, bound, split=(), held_as=jnp.bfloat16):
    array = width * jax.random.normal(stream_key, dims, jnp.float32)
    if split:
        array = array * shard_levels(stream_key, dims, split, -0.22, 0.18)
    return jnp.clip(array, -bound, bound).astype(held_as)


def setup_inputs(seed: int = 0) -> dict:
    arg_keys = jax.random.split(jax.random.key(seed), 5)
    return {
        "voltages": bell_draw(arg_keys[0], (INPUTS, SPECTRA, 2, NCHAN), 1.0, 6.0, ((0, 128), (1, 4))),
        "filter_taps": bell_draw(arg_keys[1], (TAPS, NCHAN), TAPS ** -0.5, 1.75, (), jnp.float32),
        "flagged": draw_flagged(jax.random.fold_in(arg_keys[4], 71), 0),
        "owners": draw_owners(jax.random.fold_in(arg_keys[4], 71), 0),
    }


def dft_tables(channels):
    positions = jnp.arange(channels, dtype=jnp.int32)
    phases = positions[:, None] * positions[None, :] % channels
    angles = phases.astype(jnp.float32) * (2.0 * math.pi / channels)
    factor = 1.0 / math.sqrt(channels)
    return ((jnp.cos(angles) * factor).astype(jnp.bfloat16), (jnp.sin(angles) * factor).astype(jnp.bfloat16))

def slot_table(flagged, owners, channels, capacity):
    channel_ids = jnp.arange(channels, dtype=jnp.int32)
    alive_mask = jnp.logical_not(jnp.any(flagged[:, None] == channel_ids[None, :], axis=0))
    earlier = (owners[None, :] == owners[:, None]) & alive_mask[None, :] & (channel_ids[None, :] < channel_ids[:, None])
    order_rank = lax.optimization_barrier(jnp.sum(earlier.astype(jnp.int32), axis=1))
    slot_of = owners * capacity + order_rank
    matches = (slot_of[None, :] == channel_ids[:, None]) & alive_mask[None, :]
    present = jnp.any(matches, axis=1)
    chosen = lax.optimization_barrier(jnp.sum(jnp.where(matches, channel_ids[None, :], 0), axis=1)).astype(jnp.int32)
    return (chosen, present)

def channelize(samples, filter_taps, cos_table, sin_table):
    widened = samples.astype(jnp.float32)
    padded = jnp.pad(widened, ((TAPS - 1, 0), (0, 0), (0, 0)))
    running = jnp.zeros(widened.shape, jnp.float32)
    for tap_index in range(TAPS):
        start_row = TAPS - 1 - tap_index
        running = running + filter_taps[tap_index][None, None, :] * padded[start_row:start_row + SPECTRA]
    filtered = running.astype(jnp.bfloat16)
    flat_rows = filtered.reshape(SPECTRA * 2, NCHAN)
    cos_part = jnp.dot(flat_rows, cos_table, preferred_element_type=jnp.float32).reshape(SPECTRA, 2, NCHAN)
    sin_part = jnp.dot(flat_rows, sin_table, preferred_element_type=jnp.float32).reshape(SPECTRA, 2, NCHAN)
    real_part = cos_part[:, 0] + sin_part[:, 1]
    imag_part = cos_part[:, 1] - sin_part[:, 0]
    return jnp.stack([real_part, imag_part], axis=1).astype(jnp.bfloat16)

def correlate(slot_block):
    real_part = slot_block[0]
    imag_part = slot_block[1]
    first_rows = jnp.concatenate([real_part, imag_part], axis=1)
    second_rows = jnp.concatenate([imag_part, -real_part], axis=1)
    vis_real = jnp.dot(first_rows, first_rows.T, preferred_element_type=jnp.float32)
    vis_imag = jnp.dot(second_rows, first_rows.T, preferred_element_type=jnp.float32)
    return jnp.stack([vis_real, vis_imag], axis=0) / SPECTRA

def reference(voltages, filter_taps, flagged, owners):
    cos_table, sin_table = dft_tables(NCHAN)

    def one_input(samples):
        return channelize(samples, filter_taps, cos_table, sin_table)
    spectra = lax.map(one_input, voltages)
    chosen, present = slot_table(flagged, owners, NCHAN, CAP)
    picked = jnp.take(spectra, chosen, axis=3)
    picked = jnp.where(present[None, None, None, :], picked, jnp.zeros((), jnp.bfloat16))
    per_slot = jnp.transpose(picked, (3, 2, 0, 1))
    return lax.map(correlate, per_slot)
```

```python
import math

import jax
import jax.numpy as jnp
from jax import lax
from jax.sharding import PartitionSpec as P


def from_behind(value, axis, by):
    count = lax.axis_size(axis)
    pairs = [(i, i + by) for i in range(count) if 0 <= i + by < count]
    return lax.ppermute(value, axis, pairs)


def slot_table(flagged, owners, channels, capacity):
    channel_ids = jnp.arange(channels, dtype=jnp.int32)
    alive_mask = jnp.logical_not(jnp.any(flagged[:, None] == channel_ids[None, :], axis=0))
    earlier = (
        (owners[None, :] == owners[:, None])
        & alive_mask[None, :]
        & (channel_ids[None, :] < channel_ids[:, None])
    )
    order_rank = jnp.sum(earlier.astype(jnp.int32), axis=1)
    slot_of = owners * capacity + order_rank
    matches = (slot_of[None, :] == channel_ids[:, None]) & alive_mask[None, :]
    present = jnp.any(matches, axis=1)
    chosen = jnp.sum(jnp.where(matches, channel_ids[None, :], 0), axis=1)
    return (chosen, present)


def slot_tables(chosen, present, channels):
    low = 32
    high = channels // low
    step = 2.0 * math.pi / channels
    hi = jnp.arange(high, dtype=jnp.int32)
    lo = jnp.arange(low, dtype=jnp.int32)
    phase_hi = (chosen[:, None] * (hi[None, :] * low)) % channels
    phase_lo = (chosen[:, None] * lo[None, :]) % channels
    angle_hi = phase_hi.astype(jnp.float32) * step
    angle_lo = phase_lo.astype(jnp.float32) * step
    c1, s1 = jnp.cos(angle_hi)[:, :, None], jnp.sin(angle_hi)[:, :, None]
    c2, s2 = jnp.cos(angle_lo)[:, None, :], jnp.sin(angle_lo)[:, None, :]
    factor = 1.0 / math.sqrt(channels)
    keep = jnp.where(present, factor, 0.0).astype(jnp.float32)[:, None, None]
    cos_rows = ((c1 * c2 - s1 * s2) * keep).reshape(-1, channels)
    sin_rows = ((s1 * c2 + c1 * s2) * keep).reshape(-1, channels)
    return jnp.stack([cos_rows, sin_rows]).astype(jnp.bfloat16)


def local(voltages, filter_taps, flagged, owners):
    inp_dev = voltages.shape[0]
    spec_dev = voltages.shape[1]
    channels = voltages.shape[3]
    halo_depth = filter_taps.shape[0] - 1
    tail_block = voltages[:, spec_dev - halo_depth :]
    before = from_behind(tail_block, "tm", 1)
    joined = jnp.concatenate([before, voltages], axis=1).transpose(2, 0, 1, 3)
    running = jnp.zeros((2, inp_dev, spec_dev, channels), jnp.float32)
    for tap_index in range(halo_depth + 1):
        start_row = halo_depth - tap_index
        running = running + filter_taps[tap_index][None, None, None, :] * joined[
            :, :, start_row : start_row + spec_dev
        ].astype(jnp.float32)
    filtered = running.astype(jnp.bfloat16)

    chan_count = lax.axis_size("chan")
    time_count = lax.axis_size("tm")
    devices = chan_count * time_count
    capacity = channels // devices
    chosen, present = slot_table(flagged, owners, channels, capacity)
    tables = slot_tables(chosen, present, channels)
    parts = jnp.einsum("qsn,pitn->qspit", tables, filtered, preferred_element_type=jnp.float32)
    real_part = parts[0, :, 0] + parts[1, :, 1]
    imag_part = parts[0, :, 1] - parts[1, :, 0]
    spectra = jnp.stack([real_part, imag_part], axis=1).astype(jnp.bfloat16)
    sending = spectra.reshape(devices, capacity, 2, inp_dev, spec_dev)
    received = lax.all_to_all(sending, ("chan", "tm"), 0, 0, tiled=True)
    slots = received.reshape(chan_count, time_count, capacity, 2, inp_dev, spec_dev)
    slots = slots.transpose(2, 3, 0, 4, 1, 5).reshape(
        capacity, 2, chan_count * inp_dev, time_count * spec_dev
    )
    spec_all = time_count * spec_dev
    slot_real = slots[:, 0]
    slot_imag = slots[:, 1]
    first_rows = jnp.concatenate([slot_real, slot_imag], axis=-1)
    second_rows = jnp.concatenate([slot_imag, -slot_real], axis=-1)
    stacked_rows = jnp.stack([first_rows, second_rows], axis=1)
    visibility = jnp.einsum(
        "cpit,cjt->cpij", stacked_rows, first_rows, preferred_element_type=jnp.float32
    )
    return visibility / spec_all


def solution(mesh):
    return jax.shard_map(
        local,
        mesh=mesh,
        in_specs=(P("chan", "tm", None, None), P(), P(), P()),
        out_specs=P(("chan", "tm"), None, None, None),
        check_vma=False,
    )
```

```python
import math

import jax
import jax.numpy as jnp
from jax import lax
from jax.sharding import PartitionSpec as P


def from_behind(value, axis, by):
    count = lax.axis_size(axis)
    pairs = [(i, i + by) for i in range(count) if 0 <= i + by < count]
    return lax.ppermute(value, axis, pairs)


def slot_table(flagged, owners, channels, capacity):
    channel_ids = jnp.arange(channels, dtype=jnp.int32)
    alive_mask = jnp.logical_not(jnp.any(flagged[:, None] == channel_ids[None, :], axis=0))
    earlier = (
        (owners[None, :] == owners[:, None])
        & alive_mask[None, :]
        & (channel_ids[None, :] < channel_ids[:, None])
    )
    order_rank = jnp.sum(earlier.astype(jnp.int32), axis=1)
    slot_of = owners * capacity + order_rank
    matches = (slot_of[None, :] == channel_ids[:, None]) & alive_mask[None, :]
    present = jnp.any(matches, axis=1)
    chosen = jnp.sum(jnp.where(matches, channel_ids[None, :], 0), axis=1)
    return (chosen, present)


def slot_tables(chosen, present, channels):
    low = 32
    high = channels // low
    step = 2.0 * math.pi / channels
    hi = jnp.arange(high, dtype=jnp.int32)
    lo = jnp.arange(low, dtype=jnp.int32)
    angle_hi = ((hi[:, None] * low * chosen[None, :]) % channels).astype(jnp.float32) * step
    angle_lo = ((lo[:, None] * chosen[None, :]) % channels).astype(jnp.float32) * step
    c1, s1 = jnp.cos(angle_hi)[:, None, :], jnp.sin(angle_hi)[:, None, :]
    c2, s2 = jnp.cos(angle_lo)[None, :, :], jnp.sin(angle_lo)[None, :, :]
    factor = 1.0 / math.sqrt(channels)
    keep = jnp.where(present, factor, 0.0).astype(jnp.float32)[None, None, :]
    cos_rows = ((c1 * c2 - s1 * s2) * keep).reshape(channels, -1)
    sin_rows = ((s1 * c2 + c1 * s2) * keep).reshape(channels, -1)
    return cos_rows.astype(jnp.bfloat16), sin_rows.astype(jnp.bfloat16)


def local(voltages, filter_taps, flagged, owners):
    inp_dev = voltages.shape[0]
    spec_dev = voltages.shape[1]
    channels = voltages.shape[3]
    halo_depth = filter_taps.shape[0] - 1
    tail_block = voltages[:, spec_dev - halo_depth :]
    before = from_behind(tail_block, "tm", 1)
    joined = jnp.concatenate([before, voltages], axis=1).transpose(2, 0, 1, 3)
    running = jnp.zeros((2, inp_dev, spec_dev, channels), jnp.float32)
    for tap_index in range(halo_depth + 1):
        start_row = halo_depth - tap_index
        running = running + filter_taps[tap_index][None, None, None, :] * joined[
            :, :, start_row : start_row + spec_dev
        ].astype(jnp.float32)
    filtered = running.astype(jnp.bfloat16).reshape(2, inp_dev * spec_dev, channels)

    chan_count = lax.axis_size("chan")
    time_count = lax.axis_size("tm")
    devices = chan_count * time_count
    capacity = channels // devices
    chosen, present = slot_table(flagged, owners, channels, capacity)
    cos_rows, sin_rows = slot_tables(chosen, present, channels)
    dims = (((0,), (2,)), ((), ()))
    cos_part = lax.dot_general(cos_rows, filtered, dims, preferred_element_type=jnp.float32)
    sin_part = lax.dot_general(sin_rows, filtered, dims, preferred_element_type=jnp.float32)
    real_part = cos_part[:, 0] + sin_part[:, 1]
    imag_part = cos_part[:, 1] - sin_part[:, 0]
    spectra = jnp.stack([real_part, imag_part], axis=1).astype(jnp.bfloat16)
    rows = inp_dev * spec_dev
    sending = spectra.reshape(devices, capacity * 2 * rows)
    received = lax.all_to_all(sending, ("chan", "tm"), 0, 0, tiled=True)
    slots = received.reshape(chan_count, time_count, capacity, 2, inp_dev, spec_dev)
    first_rows = slots.transpose(2, 0, 4, 3, 1, 5).reshape(
        capacity, chan_count * inp_dev, 2, time_count * spec_dev
    )
    second_rows = jnp.stack([first_rows[:, :, 1], -first_rows[:, :, 0]], axis=2)
    first_rows = first_rows.reshape(capacity, chan_count * inp_dev, -1)
    second_rows = second_rows.reshape(capacity, chan_count * inp_dev, -1)
    stacked_rows = jnp.stack([first_rows, second_rows], axis=1)
    visibility = jnp.einsum(
        "cpit,cjt->cpij", stacked_rows, first_rows, preferred_element_type=jnp.float32
    )
    return visibility / (time_count * spec_dev)


def solution(mesh):
    return jax.shard_map(
        local,
        mesh=mesh,
        in_specs=(P("chan", "tm", None, None), P(), P(), P()),
        out_specs=P(("chan", "tm"), None, None, None),
        check_vma=False,
    )
```

```python
import functools
import math

import jax
import jax.numpy as jnp
from jax import lax
from jax.experimental import pallas as pl
from jax.experimental.pallas import tpu as pltpu
from jax.sharding import PartitionSpec as P


def from_behind(value, axis, by):
    count = lax.axis_size(axis)
    pairs = [(i, i + by) for i in range(count) if 0 <= i + by < count]
    return lax.ppermute(value, axis, pairs)


def slot_table(flagged, owners, channels, capacity):
    channel_ids = jnp.arange(channels, dtype=jnp.int32)
    alive_mask = jnp.logical_not(jnp.any(flagged[:, None] == channel_ids[None, :], axis=0))
    earlier = (
        (owners[None, :] == owners[:, None])
        & alive_mask[None, :]
        & (channel_ids[None, :] < channel_ids[:, None])
    )
    order_rank = jnp.sum(earlier.astype(jnp.int32), axis=1)
    slot_of = owners * capacity + order_rank
    matches = (slot_of[None, :] == channel_ids[:, None]) & alive_mask[None, :]
    present = jnp.any(matches, axis=1)
    chosen = jnp.sum(jnp.where(matches, channel_ids[None, :], 0), axis=1)
    return (chosen, present)


def slot_tables(chosen, present, channels):
    low = 32
    high = channels // low
    step = 2.0 * math.pi / channels
    hi = jnp.arange(high, dtype=jnp.int32)
    lo = jnp.arange(low, dtype=jnp.int32)
    angle_hi = ((hi[:, None] * low * chosen[None, :]) % channels).astype(jnp.float32) * step
    angle_lo = ((lo[:, None] * chosen[None, :]) % channels).astype(jnp.float32) * step
    c1, s1 = jnp.cos(angle_hi)[:, None, :], jnp.sin(angle_hi)[:, None, :]
    c2, s2 = jnp.cos(angle_lo)[None, :, :], jnp.sin(angle_lo)[None, :, :]
    factor = 1.0 / math.sqrt(channels)
    keep = jnp.where(present, factor, 0.0).astype(jnp.float32)[None, None, :]
    cos_rows = ((c1 * c2 - s1 * s2) * keep).reshape(channels, -1)
    sin_rows = ((s1 * c2 + c1 * s2) * keep).reshape(channels, -1)
    return cos_rows.astype(jnp.bfloat16), sin_rows.astype(jnp.bfloat16)


def dft_kernel(x_ref, c0_ref, c1_ref, s0_ref, s1_ref, o_ref):
    x = x_ref[...]
    half = x.shape[0] // 2
    for cap, (c_ref, s_ref) in enumerate(((c0_ref, s0_ref), (c1_ref, s1_ref))):
        cos_part = jnp.dot(x, c_ref[...], preferred_element_type=jnp.float32)
        sin_part = jnp.dot(x, s_ref[...], preferred_element_type=jnp.float32)
        real_part = cos_part[:half] + sin_part[half:]
        imag_part = cos_part[half:] - sin_part[:half]
        o_ref[:, 2 * cap, :] = real_part.T.astype(o_ref.dtype)
        o_ref[:, 2 * cap + 1, :] = imag_part.T.astype(o_ref.dtype)


def dft_payload(filtered, cos_rows, sin_rows, devices, capacity):
    channels = filtered.shape[1]
    rows = filtered.shape[0] // 2
    block = 128
    steps = devices // block
    table_spec = lambda cap: pl.BlockSpec((channels, block), lambda j: (0, j + cap * steps))
    return pl.pallas_call(
        dft_kernel,
        grid=(steps,),
        in_specs=[
            pl.BlockSpec((2 * rows, channels), lambda j: (0, 0)),
            table_spec(0),
            table_spec(1),
            table_spec(0),
            table_spec(1),
        ],
        out_specs=pl.BlockSpec((block, capacity * 2, rows), lambda j: (j, 0, 0)),
        out_shape=jax.ShapeDtypeStruct((devices, capacity * 2, rows), jnp.bfloat16),
    )(filtered, cos_rows, cos_rows, sin_rows, sin_rows)


def local(voltages, filter_taps, flagged, owners):
    inp_dev = voltages.shape[0]
    spec_dev = voltages.shape[1]
    channels = voltages.shape[3]
    halo_depth = filter_taps.shape[0] - 1
    tail_block = voltages[:, spec_dev - halo_depth :]
    before = from_behind(tail_block, "tm", 1)
    joined = jnp.concatenate([before, voltages], axis=1).transpose(2, 0, 1, 3)
    running = jnp.zeros((2, inp_dev, spec_dev, channels), jnp.float32)
    for tap_index in range(halo_depth + 1):
        start_row = halo_depth - tap_index
        running = running + filter_taps[tap_index][None, None, None, :] * joined[
            :, :, start_row : start_row + spec_dev
        ].astype(jnp.float32)
    filtered = running.astype(jnp.bfloat16).reshape(2 * inp_dev * spec_dev, channels)

    chan_count = lax.axis_size("chan")
    time_count = lax.axis_size("tm")
    devices = chan_count * time_count
    capacity = channels // devices
    chosen, present = slot_table(flagged, owners, channels, capacity)
    chosen = chosen.reshape(chan_count, time_count, capacity).transpose(2, 1, 0).reshape(-1)
    present = present.reshape(chan_count, time_count, capacity).transpose(2, 1, 0).reshape(-1)
    cos_rows, sin_rows = slot_tables(chosen, present, channels)
    sending = dft_payload(filtered, cos_rows, sin_rows, devices, capacity)
    received = lax.all_to_all(sending, ("tm", "chan"), 0, 0, tiled=True)
    return correlate(received, time_count, chan_count, capacity, inp_dev)


def correlate_kernel(r_ref, o_ref, xt_ref, *, time_count, inp_dev, caps):
    for cap in range(caps):
        pl.when(pl.program_id(0) == cap)(
            functools.partial(correlate_slot, r_ref, o_ref, xt_ref, cap, time_count, inp_dev)
        )


def correlate_slot(r_ref, o_ref, xt_ref, cap, time_count, inp_dev):
    chans = r_ref.shape[0] // time_count
    spec_dev = r_ref.shape[2] // inp_dev
    for reim in range(2):
        for tm in range(time_count):
            piece = r_ref[pl.ds(tm * chans, chans), cap * 2 + reim, :]
            block = piece.astype(jnp.float32).T
            row = (reim * time_count + tm) * spec_dev
            for i in range(inp_dev):
                xt_ref[row : row + spec_dev, i * chans : (i + 1) * chans] = block[
                    i * spec_dev : (i + 1) * spec_dev
                ]
    inputs = inp_dev * chans
    rows = lax.broadcasted_iota(jnp.int32, (inputs, inputs), 0)
    cols = lax.broadcasted_iota(jnp.int32, (inputs, inputs), 1)
    perm = (cols == (rows % inp_dev) * chans + rows // inp_dev).astype(jnp.bfloat16)
    nt = (((1,), (1,)), ((), ()))
    xt = xt_ref[...].astype(jnp.bfloat16)
    x = lax.dot_general(perm, xt, nt, preferred_element_type=jnp.float32).astype(jnp.bfloat16)
    half = x.shape[1] // 2
    x2 = jnp.concatenate([x[:, half:], -x[:, :half]], axis=1)
    scale = 1.0 / (time_count * spec_dev)
    o_ref[0, 0] = lax.dot_general(x, x, nt, preferred_element_type=jnp.float32) * scale
    o_ref[0, 1] = lax.dot_general(x2, x, nt, preferred_element_type=jnp.float32) * scale


def correlate(received, time_count, chan_count, capacity, inp_dev):
    width = received.shape[2]
    spec_dev = width // inp_dev
    inputs = chan_count * inp_dev
    kernel = functools.partial(correlate_kernel, time_count=time_count, inp_dev=inp_dev, caps=capacity)
    return pl.pallas_call(
        kernel,
        grid=(capacity,),
        in_specs=[pl.BlockSpec(received.shape, lambda c: (0, 0, 0))],
        out_specs=pl.BlockSpec((1, 2, inputs, inputs), lambda c: (c, 0, 0, 0)),
        out_shape=jax.ShapeDtypeStruct((capacity, 2, inputs, inputs), jnp.float32),
        scratch_shapes=[pltpu.VMEM((2 * time_count * spec_dev, inputs), jnp.float32)],
    )(received)


def solution(mesh):
    return jax.shard_map(
        local,
        mesh=mesh,
        in_specs=(P("chan", "tm", None, None), P(), P(), P()),
        out_specs=P(("chan", "tm"), None, None, None),
        check_vma=False,
    )
```

```python
import functools
import math

import jax
import jax.numpy as jnp
from jax import lax
from jax.experimental import pallas as pl
from jax.experimental.pallas import tpu as pltpu
from jax.sharding import PartitionSpec as P


def from_behind(value, axis, by):
    count = lax.axis_size(axis)
    pairs = [(i, i + by) for i in range(count) if 0 <= i + by < count]
    return lax.ppermute(value, axis, pairs)


def slot_table(flagged, owners, channels, devices):
    channel_ids = jnp.arange(channels, dtype=jnp.int32)
    alive_mask = jnp.logical_not(jnp.any(flagged[:, None] == channel_ids[None, :], axis=0))
    device_ids = jnp.arange(devices, dtype=jnp.int32)
    mine = (owners[None, :] == device_ids[:, None]) & alive_mask[None, :]
    count = jnp.sum(mine.astype(jnp.int32), axis=1)
    lower = jnp.min(jnp.where(mine, channel_ids[None, :], channels), axis=1)
    upper = jnp.max(jnp.where(mine, channel_ids[None, :], 0), axis=1)
    chosen = jnp.stack([jnp.where(count > 0, lower, 0), jnp.where(count > 1, upper, 0)], axis=1)
    present = jnp.stack([count > 0, count > 1], axis=1)
    return (chosen.reshape(-1), present.reshape(-1))


def slot_tables(chosen, present, channels):
    low = 32
    high = channels // low
    step = 2.0 * math.pi / channels
    hi = jnp.arange(high, dtype=jnp.int32)
    lo = jnp.arange(low, dtype=jnp.int32)
    angle_hi = ((hi[:, None] * low * chosen[None, :]) % channels).astype(jnp.float32) * step
    angle_lo = ((lo[:, None] * chosen[None, :]) % channels).astype(jnp.float32) * step
    c1, s1 = jnp.cos(angle_hi)[:, None, :], jnp.sin(angle_hi)[:, None, :]
    c2, s2 = jnp.cos(angle_lo)[None, :, :], jnp.sin(angle_lo)[None, :, :]
    factor = 1.0 / math.sqrt(channels)
    keep = jnp.where(present, factor, 0.0).astype(jnp.float32)[None, None, :]
    cos_rows = ((c1 * c2 - s1 * s2) * keep).reshape(channels, -1)
    sin_rows = ((s1 * c2 + c1 * s2) * keep).reshape(channels, -1)
    return cos_rows.astype(jnp.bfloat16), sin_rows.astype(jnp.bfloat16)


def dft_kernel(x_ref, c0_ref, c1_ref, s0_ref, s1_ref, o_ref):
    x = x_ref[...]
    half = x.shape[0] // 2
    for cap, (c_ref, s_ref) in enumerate(((c0_ref, s0_ref), (c1_ref, s1_ref))):
        cos_part = jnp.dot(x, c_ref[...], preferred_element_type=jnp.float32)
        sin_part = jnp.dot(x, s_ref[...], preferred_element_type=jnp.float32)
        real_part = cos_part[:half] + sin_part[half:]
        imag_part = cos_part[half:] - sin_part[:half]
        o_ref[:, 2 * cap, :] = real_part.T.astype(o_ref.dtype)
        o_ref[:, 2 * cap + 1, :] = imag_part.T.astype(o_ref.dtype)


def dft_payload(filtered, cos_rows, sin_rows, devices, capacity):
    channels = filtered.shape[1]
    rows = filtered.shape[0] // 2
    block = 256
    steps = devices // block
    table_spec = lambda cap: pl.BlockSpec((channels, block), lambda j: (0, j + cap * steps))
    return pl.pallas_call(
        dft_kernel,
        grid=(steps,),
        in_specs=[
            pl.BlockSpec((2 * rows, channels), lambda j: (0, 0)),
            table_spec(0),
            table_spec(1),
            table_spec(0),
            table_spec(1),
        ],
        out_specs=pl.BlockSpec((block, capacity * 2, rows), lambda j: (j, 0, 0)),
        out_shape=jax.ShapeDtypeStruct((devices, capacity * 2, rows), jnp.bfloat16),
    )(filtered, cos_rows, cos_rows, sin_rows, sin_rows)


def local(voltages, filter_taps, flagged, owners):
    inp_dev = voltages.shape[0]
    spec_dev = voltages.shape[1]
    channels = voltages.shape[3]
    halo_depth = filter_taps.shape[0] - 1
    tail_block = voltages[:, spec_dev - halo_depth :]
    before = from_behind(tail_block, "tm", 1)
    joined = jnp.concatenate([before, voltages], axis=1).transpose(2, 0, 1, 3)
    running = jnp.zeros((2, inp_dev, spec_dev, channels), jnp.float32)
    for tap_index in range(halo_depth + 1):
        start_row = halo_depth - tap_index
        running = running + filter_taps[tap_index][None, None, None, :] * joined[
            :, :, start_row : start_row + spec_dev
        ].astype(jnp.float32)
    filtered = running.astype(jnp.bfloat16).reshape(2 * inp_dev * spec_dev, channels)

    chan_count = lax.axis_size("chan")
    time_count = lax.axis_size("tm")
    devices = chan_count * time_count
    capacity = channels // devices
    chosen, present = slot_table(flagged, owners, channels, devices)
    chosen = chosen.reshape(chan_count, time_count, capacity).transpose(2, 1, 0).reshape(-1)
    present = present.reshape(chan_count, time_count, capacity).transpose(2, 1, 0).reshape(-1)
    cos_rows, sin_rows = slot_tables(chosen, present, channels)
    sending = dft_payload(filtered, cos_rows, sin_rows, devices, capacity)
    received = lax.all_to_all(sending, ("tm", "chan"), 0, 0, tiled=True)
    return correlate(received, time_count, chan_count, capacity, inp_dev)


def correlate_kernel(r_ref, o_ref, xt_ref, *, time_count, inp_dev, caps):
    for cap in range(caps):
        pl.when(pl.program_id(0) == cap)(
            functools.partial(correlate_slot, r_ref, o_ref, xt_ref, cap, time_count, inp_dev)
        )


def correlate_slot(r_ref, o_ref, xt_ref, cap, time_count, inp_dev):
    chans = r_ref.shape[0] // time_count
    spec_dev = r_ref.shape[2] // inp_dev
    for reim in range(2):
        for tm in range(time_count):
            piece = r_ref[pl.ds(tm * chans, chans), cap * 2 + reim, :]
            block = piece.astype(jnp.float32).T
            row = (reim * time_count + tm) * spec_dev
            for i in range(inp_dev):
                xt_ref[row : row + spec_dev, i * chans : (i + 1) * chans] = block[
                    i * spec_dev : (i + 1) * spec_dev
                ]
    inputs = inp_dev * chans
    rows = lax.broadcasted_iota(jnp.int32, (inputs, inputs), 0)
    cols = lax.broadcasted_iota(jnp.int32, (inputs, inputs), 1)
    perm = (cols == (rows % inp_dev) * chans + rows // inp_dev).astype(jnp.bfloat16)
    nt = (((1,), (1,)), ((), ()))
    xt = xt_ref[...].astype(jnp.bfloat16)
    x = lax.dot_general(perm, xt, nt, preferred_element_type=jnp.float32).astype(jnp.bfloat16)
    half = x.shape[1] // 2
    x2 = jnp.concatenate([x[:, half:], -x[:, :half]], axis=1)
    scale = 1.0 / (time_count * spec_dev)
    o_ref[0, 0] = lax.dot_general(x, x, nt, preferred_element_type=jnp.float32) * scale
    o_ref[0, 1] = lax.dot_general(x2, x, nt, preferred_element_type=jnp.float32) * scale


def correlate(received, time_count, chan_count, capacity, inp_dev):
    width = received.shape[2]
    spec_dev = width // inp_dev
    inputs = chan_count * inp_dev
    kernel = functools.partial(correlate_kernel, time_count=time_count, inp_dev=inp_dev, caps=capacity)
    return pl.pallas_call(
        kernel,
        grid=(capacity,),
        in_specs=[pl.BlockSpec(received.shape, lambda c: (0, 0, 0))],
        out_specs=pl.BlockSpec((1, 2, inputs, inputs), lambda c: (c, 0, 0, 0)),
        out_shape=jax.ShapeDtypeStruct((capacity, 2, inputs, inputs), jnp.float32),
        scratch_shapes=[pltpu.VMEM((2 * time_count * spec_dev, inputs), jnp.float32)],
    )(received)


def solution(mesh):
    return jax.shard_map(
        local,
        mesh=mesh,
        in_specs=(P("chan", "tm", None, None), P(), P(), P()),
        out_specs=P(("chan", "tm"), None, None, None),
        check_vma=False,
    )
```

```python
import functools
import math

import jax
import jax.numpy as jnp
from jax import lax
from jax.experimental import pallas as pl
from jax.experimental.pallas import tpu as pltpu
from jax.sharding import PartitionSpec as P


def from_behind(value, axis, by):
    count = lax.axis_size(axis)
    pairs = [(i, i + by) for i in range(count) if 0 <= i + by < count]
    return lax.ppermute(value, axis, pairs)


def slot_table(flagged, owners, channels, devices):
    channel_ids = jnp.arange(channels, dtype=jnp.int32)
    alive_mask = jnp.logical_not(jnp.any(flagged[:, None] == channel_ids[None, :], axis=0))
    device_ids = jnp.arange(devices, dtype=jnp.int32)
    mine = (owners[None, :] == device_ids[:, None]) & alive_mask[None, :]
    count = jnp.sum(mine.astype(jnp.int32), axis=1)
    lower = jnp.min(jnp.where(mine, channel_ids[None, :], channels), axis=1)
    upper = jnp.max(jnp.where(mine, channel_ids[None, :], 0), axis=1)
    chosen = jnp.stack([jnp.where(count > 0, lower, 0), jnp.where(count > 1, upper, 0)], axis=1)
    present = jnp.stack([count > 0, count > 1], axis=1)
    return (chosen.reshape(-1), present.reshape(-1))


def slot_factors(chosen, present, channels, lanes):
    step = 2.0 * math.pi / channels
    high = jnp.arange(channels // lanes, dtype=jnp.int32)
    low = jnp.arange(lanes, dtype=jnp.int32)
    angle_hi = ((chosen[:, None] * (high[None, :] * lanes)) % channels).astype(jnp.float32) * step
    angle_lo = ((chosen[:, None] * low[None, :]) % channels).astype(jnp.float32) * step
    keep = jnp.where(present, 1.0 / math.sqrt(channels), 0.0).astype(jnp.float32)[:, None]
    return (jnp.cos(angle_hi), jnp.sin(angle_hi), jnp.cos(angle_lo) * keep, jnp.sin(angle_lo) * keep)


def dft_kernel(x_ref, *refs):
    factor_refs, o_ref = refs[:-1], refs[-1]
    x = x_ref[...]
    half = x.shape[0] // 2
    nt = (((1,), (1,)), ((), ()))
    for cap in range(len(factor_refs) // 4):
        cv, sv, cl, sl = (r[...] for r in factor_refs[4 * cap : 4 * cap + 4])
        cos_tiles = []
        sin_tiles = []
        for v in range(cv.shape[1]):
            cv_v = cv[:, v : v + 1]
            sv_v = sv[:, v : v + 1]
            cos_tiles.append(cv_v * cl - sv_v * sl)
            sin_tiles.append(sv_v * cl + cv_v * sl)
        cos_rows = jnp.concatenate(cos_tiles, axis=1).astype(jnp.bfloat16)
        sin_rows = jnp.concatenate(sin_tiles, axis=1).astype(jnp.bfloat16)
        cos_part = lax.dot_general(cos_rows, x, nt, preferred_element_type=jnp.float32)
        sin_part = lax.dot_general(sin_rows, x, nt, preferred_element_type=jnp.float32)
        o_ref[:, 2 * cap, :] = (cos_part[:, :half] + sin_part[:, half:]).astype(o_ref.dtype)
        o_ref[:, 2 * cap + 1, :] = (cos_part[:, half:] - sin_part[:, :half]).astype(o_ref.dtype)


def dft_payload(filtered, factors, devices, capacity):
    channels = filtered.shape[1]
    rows = filtered.shape[0] // 2
    block = 256
    steps = devices // block
    specs = []
    operands = []
    for cap in range(capacity):
        for f in factors:
            specs.append(pl.BlockSpec((block, f.shape[1]), lambda j, cap=cap: (j + cap * steps, 0)))
            operands.append(f)
    return pl.pallas_call(
        dft_kernel,
        grid=(steps,),
        in_specs=[pl.BlockSpec((2 * rows, channels), lambda j: (0, 0))] + specs,
        out_specs=pl.BlockSpec((block, capacity * 2, rows), lambda j: (j, 0, 0)),
        out_shape=jax.ShapeDtypeStruct((devices, capacity * 2, rows), jnp.bfloat16),
    )(filtered, *operands)


def local(voltages, filter_taps, flagged, owners):
    inp_dev = voltages.shape[0]
    spec_dev = voltages.shape[1]
    channels = voltages.shape[3]
    halo_depth = filter_taps.shape[0] - 1
    tail_block = voltages[:, spec_dev - halo_depth :]
    before = from_behind(tail_block, "tm", 1)
    joined = jnp.concatenate([before, voltages], axis=1).transpose(2, 0, 1, 3)
    running = jnp.zeros((2, inp_dev, spec_dev, channels), jnp.float32)
    for tap_index in range(halo_depth + 1):
        start_row = halo_depth - tap_index
        running = running + filter_taps[tap_index][None, None, None, :] * joined[
            :, :, start_row : start_row + spec_dev
        ].astype(jnp.float32)
    filtered = running.astype(jnp.bfloat16).reshape(2 * inp_dev * spec_dev, channels)

    chan_count = lax.axis_size("chan")
    time_count = lax.axis_size("tm")
    devices = chan_count * time_count
    capacity = channels // devices
    chosen, present = slot_table(flagged, owners, channels, devices)
    chosen = chosen.reshape(chan_count, time_count, capacity).transpose(2, 1, 0).reshape(-1)
    present = present.reshape(chan_count, time_count, capacity).transpose(2, 1, 0).reshape(-1)
    factors = slot_factors(chosen, present, channels, 128)
    sending = dft_payload(filtered, factors, devices, capacity)
    received = lax.all_to_all(sending, ("tm", "chan"), 0, 0, tiled=True)
    return correlate(received, time_count, chan_count, capacity, inp_dev)


def correlate_kernel(r_ref, o_ref, xt_ref, *, time_count, inp_dev, caps):
    for cap in range(caps):
        pl.when(pl.program_id(0) == cap)(
            functools.partial(correlate_slot, r_ref, o_ref, xt_ref, cap, time_count, inp_dev)
        )


def correlate_slot(r_ref, o_ref, xt_ref, cap, time_count, inp_dev):
    chans = r_ref.shape[0] // time_count
    spec_dev = r_ref.shape[2] // inp_dev
    for reim in range(2):
        for tm in range(time_count):
            piece = r_ref[pl.ds(tm * chans, chans), cap * 2 + reim, :]
            block = piece.astype(jnp.float32).T
            row = (reim * time_count + tm) * spec_dev
            for i in range(inp_dev):
                xt_ref[row : row + spec_dev, i * chans : (i + 1) * chans] = block[
                    i * spec_dev : (i + 1) * spec_dev
                ]
    inputs = inp_dev * chans
    rows = lax.broadcasted_iota(jnp.int32, (inputs, inputs), 0)
    cols = lax.broadcasted_iota(jnp.int32, (inputs, inputs), 1)
    perm = (cols == (rows % inp_dev) * chans + rows // inp_dev).astype(jnp.bfloat16)
    nt = (((1,), (1,)), ((), ()))
    xt = xt_ref[...].astype(jnp.bfloat16)
    x = lax.dot_general(perm, xt, nt, preferred_element_type=jnp.float32).astype(jnp.bfloat16)
    half = x.shape[1] // 2
    x2 = jnp.concatenate([x[:, half:], -x[:, :half]], axis=1)
    scale = 1.0 / (time_count * spec_dev)
    o_ref[0, 0] = lax.dot_general(x, x, nt, preferred_element_type=jnp.float32) * scale
    o_ref[0, 1] = lax.dot_general(x2, x, nt, preferred_element_type=jnp.float32) * scale


def correlate(received, time_count, chan_count, capacity, inp_dev):
    width = received.shape[2]
    spec_dev = width // inp_dev
    inputs = chan_count * inp_dev
    kernel = functools.partial(correlate_kernel, time_count=time_count, inp_dev=inp_dev, caps=capacity)
    return pl.pallas_call(
        kernel,
        grid=(capacity,),
        in_specs=[pl.BlockSpec(received.shape, lambda c: (0, 0, 0))],
        out_specs=pl.BlockSpec((1, 2, inputs, inputs), lambda c: (c, 0, 0, 0)),
        out_shape=jax.ShapeDtypeStruct((capacity, 2, inputs, inputs), jnp.float32),
        scratch_shapes=[pltpu.VMEM((2 * time_count * spec_dev, inputs), jnp.float32)],
    )(received)


def solution(mesh):
    return jax.shard_map(
        local,
        mesh=mesh,
        in_specs=(P("chan", "tm", None, None), P(), P(), P()),
        out_specs=P(("chan", "tm"), None, None, None),
        check_vma=False,
    )
```

```python
import functools
import math

import jax
import jax.numpy as jnp
from jax import lax
from jax.experimental import pallas as pl
from jax.experimental.pallas import tpu as pltpu
from jax.sharding import PartitionSpec as P


def from_behind(value, axis, by):
    count = lax.axis_size(axis)
    pairs = [(i, i + by) for i in range(count) if 0 <= i + by < count]
    return lax.ppermute(value, axis, pairs)


def slot_table(flagged, owners, channels, devices):
    channel_ids = jnp.arange(channels, dtype=jnp.int32)
    alive_mask = jnp.logical_not(jnp.any(flagged[:, None] == channel_ids[None, :], axis=0))
    device_ids = jnp.arange(devices, dtype=jnp.int32)
    mine = (owners[None, :] == device_ids[:, None]) & alive_mask[None, :]
    count = jnp.sum(mine.astype(jnp.int32), axis=1)
    lower = jnp.min(jnp.where(mine, channel_ids[None, :], channels), axis=1)
    upper = jnp.max(jnp.where(mine, channel_ids[None, :], 0), axis=1)
    chosen = jnp.stack([jnp.where(count > 0, lower, 0), jnp.where(count > 1, upper, 0)], axis=1)
    present = jnp.stack([count > 0, count > 1], axis=1)
    return (chosen.reshape(-1), present.reshape(-1))


def slot_tables(chosen, present, channels):
    low = 32
    high = channels // low
    step = 2.0 * math.pi / channels
    hi = jnp.arange(high, dtype=jnp.int32)
    lo = jnp.arange(low, dtype=jnp.int32)
    angle_hi = ((hi[:, None] * low * chosen[None, :]) % channels).astype(jnp.float32) * step
    angle_lo = ((lo[:, None] * chosen[None, :]) % channels).astype(jnp.float32) * step
    c1, s1 = jnp.cos(angle_hi)[:, None, :], jnp.sin(angle_hi)[:, None, :]
    c2, s2 = jnp.cos(angle_lo)[None, :, :], jnp.sin(angle_lo)[None, :, :]
    factor = 1.0 / math.sqrt(channels)
    keep = jnp.where(present, factor, 0.0).astype(jnp.float32)[None, None, :]
    cos_rows = ((c1 * c2 - s1 * s2) * keep).reshape(channels, -1)
    sin_rows = ((s1 * c2 + c1 * s2) * keep).reshape(channels, -1)
    return cos_rows.astype(jnp.bfloat16), sin_rows.astype(jnp.bfloat16)


def dft_kernel(x_ref, c0_ref, c1_ref, s0_ref, s1_ref, o_ref):
    x = x_ref[...]
    half = x.shape[0] // 2
    for cap, (c_ref, s_ref) in enumerate(((c0_ref, s0_ref), (c1_ref, s1_ref))):
        cos_part = jnp.dot(x, c_ref[...], preferred_element_type=jnp.float32)
        sin_part = jnp.dot(x, s_ref[...], preferred_element_type=jnp.float32)
        real_part = cos_part[:half] + sin_part[half:]
        imag_part = cos_part[half:] - sin_part[:half]
        o_ref[:, 2 * cap, :] = real_part.T.astype(o_ref.dtype)
        o_ref[:, 2 * cap + 1, :] = imag_part.T.astype(o_ref.dtype)


def dft_payload(filtered, cos_rows, sin_rows, devices, capacity):
    channels = filtered.shape[1]
    rows = filtered.shape[0] // 2
    block = 256
    steps = devices // block
    table_spec = lambda cap: pl.BlockSpec((channels, block), lambda j: (0, j + cap * steps))
    return pl.pallas_call(
        dft_kernel,
        grid=(steps,),
        in_specs=[
            pl.BlockSpec((2 * rows, channels), lambda j: (0, 0)),
            table_spec(0),
            table_spec(1),
            table_spec(0),
            table_spec(1),
        ],
        out_specs=pl.BlockSpec((block, capacity * 2, rows), lambda j: (j, 0, 0)),
        out_shape=jax.ShapeDtypeStruct((devices, capacity * 2, rows), jnp.bfloat16),
    )(filtered, cos_rows, cos_rows, sin_rows, sin_rows)


def local(voltages, filter_taps, flagged, owners):
    inp_dev = voltages.shape[0]
    spec_dev = voltages.shape[1]
    channels = voltages.shape[3]
    halo_depth = filter_taps.shape[0] - 1
    tail_block = voltages[:, spec_dev - halo_depth :]
    before = from_behind(tail_block, "tm", 1)
    joined = jnp.concatenate([before, voltages], axis=1).transpose(2, 0, 1, 3)
    running = jnp.zeros((2, inp_dev, spec_dev, channels), jnp.float32)
    for tap_index in range(halo_depth + 1):
        start_row = halo_depth - tap_index
        running = running + filter_taps[tap_index][None, None, None, :] * joined[
            :, :, start_row : start_row + spec_dev
        ].astype(jnp.float32)
    filtered = running.astype(jnp.bfloat16).reshape(2 * inp_dev * spec_dev, channels)

    chan_count = lax.axis_size("chan")
    time_count = lax.axis_size("tm")
    devices = chan_count * time_count
    capacity = channels // devices
    chosen, present = slot_table(flagged, owners, channels, devices)
    chosen = chosen.reshape(chan_count, time_count, capacity).transpose(2, 1, 0).reshape(-1)
    present = present.reshape(chan_count, time_count, capacity).transpose(2, 1, 0).reshape(-1)
    cos_rows, sin_rows = slot_tables(chosen, present, channels)
    sending = dft_payload(filtered, cos_rows, sin_rows, devices, capacity)
    received = lax.all_to_all(sending, ("tm", "chan"), 0, 0, tiled=True)
    return correlate(received, time_count, chan_count, capacity, inp_dev)


def correlate_kernel(r_ref, o_ref, xt_ref, x_ref, x2_ref, *, time_count, inp_dev, caps):
    for cap in range(caps):
        pl.when((pl.program_id(0) == cap) & (pl.program_id(1) == 0))(
            functools.partial(gather_slot, r_ref, xt_ref, x_ref, x2_ref, cap, time_count, inp_dev)
        )
    block = o_ref.shape[2]
    start = pl.multiple_of(pl.program_id(1) * block, block)
    nt = (((1,), (1,)), ((), ()))
    scale = 1.0 / (time_count * (r_ref.shape[2] // inp_dev))
    x = x_ref[...]
    o_ref[0, 0] = lax.dot_general(x_ref[pl.ds(start, block), :], x, nt, preferred_element_type=jnp.float32) * scale
    o_ref[0, 1] = lax.dot_general(x2_ref[pl.ds(start, block), :], x, nt, preferred_element_type=jnp.float32) * scale


def gather_slot(r_ref, xt_ref, x_ref, x2_ref, cap, time_count, inp_dev):
    chans = r_ref.shape[0] // time_count
    spec_dev = r_ref.shape[2] // inp_dev
    for reim in range(2):
        for tm in range(time_count):
            piece = r_ref[pl.ds(tm * chans, chans), cap * 2 + reim, :]
            block = piece.astype(jnp.float32).T
            row = (reim * time_count + tm) * spec_dev
            for i in range(inp_dev):
                xt_ref[row : row + spec_dev, i * chans : (i + 1) * chans] = block[
                    i * spec_dev : (i + 1) * spec_dev
                ]
    inputs = inp_dev * chans
    rows = lax.broadcasted_iota(jnp.int32, (inputs, inputs), 0)
    cols = lax.broadcasted_iota(jnp.int32, (inputs, inputs), 1)
    perm = (cols == (rows % inp_dev) * chans + rows // inp_dev).astype(jnp.bfloat16)
    nt = (((1,), (1,)), ((), ()))
    xt = xt_ref[...].astype(jnp.bfloat16)
    x = lax.dot_general(perm, xt, nt, preferred_element_type=jnp.float32).astype(jnp.bfloat16)
    half = x.shape[1] // 2
    x_ref[...] = x
    x2_ref[...] = jnp.concatenate([x[:, half:], -x[:, :half]], axis=1)


def correlate(received, time_count, chan_count, capacity, inp_dev):
    width = received.shape[2]
    spec_dev = width // inp_dev
    inputs = chan_count * inp_dev
    block = 128
    kernel = functools.partial(correlate_kernel, time_count=time_count, inp_dev=inp_dev, caps=capacity)
    return pl.pallas_call(
        kernel,
        grid=(capacity, inputs // block),
        in_specs=[pl.BlockSpec(received.shape, lambda c, r: (0, 0, 0))],
        out_specs=pl.BlockSpec((1, 2, block, inputs), lambda c, r: (c, 0, r, 0)),
        out_shape=jax.ShapeDtypeStruct((capacity, 2, inputs, inputs), jnp.float32),
        scratch_shapes=[
            pltpu.VMEM((2 * time_count * spec_dev, inputs), jnp.float32),
            pltpu.VMEM((inputs, 2 * time_count * spec_dev), jnp.bfloat16),
            pltpu.VMEM((inputs, 2 * time_count * spec_dev), jnp.bfloat16),
        ],
    )(received)


def solution(mesh):
    return jax.shard_map(
        local,
        mesh=mesh,
        in_specs=(P("chan", "tm", None, None), P(), P(), P()),
        out_specs=P(("chan", "tm"), None, None, None),
        check_vma=False,
    )
```

```python
import functools
import math

import jax
import jax.numpy as jnp
from jax import lax
from jax.experimental import pallas as pl
from jax.experimental.pallas import tpu as pltpu
from jax.sharding import PartitionSpec as P


def from_behind(value, axis, by):
    count = lax.axis_size(axis)
    pairs = [(i, i + by) for i in range(count) if 0 <= i + by < count]
    return lax.ppermute(value, axis, pairs)


def slot_table(flagged, owners, channels, devices):
    channel_ids = jnp.arange(channels, dtype=jnp.int32)
    alive_mask = jnp.logical_not(jnp.any(flagged[:, None] == channel_ids[None, :], axis=0))
    device_ids = jnp.arange(devices, dtype=jnp.int32)
    mine = (owners[None, :] == device_ids[:, None]) & alive_mask[None, :]
    count = jnp.sum(mine.astype(jnp.int32), axis=1)
    lower = jnp.min(jnp.where(mine, channel_ids[None, :], channels), axis=1)
    upper = jnp.max(jnp.where(mine, channel_ids[None, :], 0), axis=1)
    chosen = jnp.stack([jnp.where(count > 0, lower, 0), jnp.where(count > 1, upper, 0)], axis=1)
    present = jnp.stack([count > 0, count > 1], axis=1)
    return (chosen.reshape(-1), present.reshape(-1))


def slot_tables(chosen, present, channels):
    low = 32
    high = channels // low
    step = 2.0 * math.pi / channels
    hi = jnp.arange(high, dtype=jnp.int32)
    lo = jnp.arange(low, dtype=jnp.int32)
    angle_hi = ((hi[:, None] * low * chosen[None, :]) % channels).astype(jnp.float32) * step
    angle_lo = ((lo[:, None] * chosen[None, :]) % channels).astype(jnp.float32) * step
    c1, s1 = jnp.cos(angle_hi)[:, None, :], jnp.sin(angle_hi)[:, None, :]
    c2, s2 = jnp.cos(angle_lo)[None, :, :], jnp.sin(angle_lo)[None, :, :]
    factor = 1.0 / math.sqrt(channels)
    keep = jnp.where(present, factor, 0.0).astype(jnp.float32)[None, None, :]
    cos_rows = ((c1 * c2 - s1 * s2) * keep).reshape(channels, -1)
    sin_rows = ((s1 * c2 + c1 * s2) * keep).reshape(channels, -1)
    return cos_rows.astype(jnp.bfloat16), sin_rows.astype(jnp.bfloat16)


def dft_kernel(x_ref, c0_ref, c1_ref, s0_ref, s1_ref, o_ref):
    x = x_ref[...]
    half = x.shape[0] // 2
    for cap, (c_ref, s_ref) in enumerate(((c0_ref, s0_ref), (c1_ref, s1_ref))):
        cos_part = jnp.dot(x, c_ref[...], preferred_element_type=jnp.float32)
        sin_part = jnp.dot(x, s_ref[...], preferred_element_type=jnp.float32)
        real_part = cos_part[:half] + sin_part[half:]
        imag_part = cos_part[half:] - sin_part[:half]
        o_ref[:, 2 * cap, :] = real_part.T.astype(o_ref.dtype)
        o_ref[:, 2 * cap + 1, :] = imag_part.T.astype(o_ref.dtype)


def dft_payload(filtered, cos_rows, sin_rows, devices, capacity):
    channels = filtered.shape[1]
    rows = filtered.shape[0] // 2
    block = 512
    steps = devices // block
    table_spec = lambda cap: pl.BlockSpec((channels, block), lambda j: (0, j + cap * steps))
    return pl.pallas_call(
        dft_kernel,
        grid=(steps,),
        in_specs=[
            pl.BlockSpec((2 * rows, channels), lambda j: (0, 0)),
            table_spec(0),
            table_spec(1),
            table_spec(0),
            table_spec(1),
        ],
        out_specs=pl.BlockSpec((block, capacity * 2, rows), lambda j: (j, 0, 0)),
        out_shape=jax.ShapeDtypeStruct((devices, capacity * 2, rows), jnp.bfloat16),
    )(filtered, cos_rows, cos_rows, sin_rows, sin_rows)


def local(voltages, filter_taps, flagged, owners):
    inp_dev = voltages.shape[0]
    spec_dev = voltages.shape[1]
    channels = voltages.shape[3]
    halo_depth = filter_taps.shape[0] - 1
    tail_block = voltages[:, spec_dev - halo_depth :]
    before = from_behind(tail_block, "tm", 1)
    joined = jnp.concatenate([before, voltages], axis=1).transpose(2, 0, 1, 3)
    running = jnp.zeros((2, inp_dev, spec_dev, channels), jnp.float32)
    for tap_index in range(halo_depth + 1):
        start_row = halo_depth - tap_index
        running = running + filter_taps[tap_index][None, None, None, :] * joined[
            :, :, start_row : start_row + spec_dev
        ].astype(jnp.float32)
    filtered = running.astype(jnp.bfloat16).reshape(2 * inp_dev * spec_dev, channels)

    chan_count = lax.axis_size("chan")
    time_count = lax.axis_size("tm")
    devices = chan_count * time_count
    capacity = channels // devices
    chosen, present = slot_table(flagged, owners, channels, devices)
    chosen = chosen.reshape(chan_count, time_count, capacity).transpose(2, 1, 0).reshape(-1)
    present = present.reshape(chan_count, time_count, capacity).transpose(2, 1, 0).reshape(-1)
    cos_rows, sin_rows = slot_tables(chosen, present, channels)
    sending = dft_payload(filtered, cos_rows, sin_rows, devices, capacity)
    received = lax.all_to_all(sending, ("tm", "chan"), 0, 0, tiled=True)
    return correlate(received, time_count, chan_count, capacity, inp_dev)


def correlate_kernel(r_ref, o_ref, xt_ref, *, time_count, inp_dev, caps):
    for cap in range(caps):
        pl.when(pl.program_id(0) == cap)(
            functools.partial(correlate_slot, r_ref, o_ref, xt_ref, cap, time_count, inp_dev)
        )


def correlate_slot(r_ref, o_ref, xt_ref, cap, time_count, inp_dev):
    chans = r_ref.shape[0] // time_count
    spec_dev = r_ref.shape[2] // inp_dev
    for reim in range(2):
        for tm in range(time_count):
            piece = r_ref[pl.ds(tm * chans, chans), cap * 2 + reim, :]
            block = piece.astype(jnp.float32).T
            row = (reim * time_count + tm) * spec_dev
            for i in range(inp_dev):
                xt_ref[row : row + spec_dev, i * chans : (i + 1) * chans] = block[
                    i * spec_dev : (i + 1) * spec_dev
                ]
    inputs = inp_dev * chans
    rows = lax.broadcasted_iota(jnp.int32, (inputs, inputs), 0)
    cols = lax.broadcasted_iota(jnp.int32, (inputs, inputs), 1)
    perm = (cols == (rows % inp_dev) * chans + rows // inp_dev).astype(jnp.bfloat16)
    nt = (((1,), (1,)), ((), ()))
    xt = xt_ref[...].astype(jnp.bfloat16)
    x = lax.dot_general(perm, xt, nt, preferred_element_type=jnp.float32).astype(jnp.bfloat16)
    half = x.shape[1] // 2
    x2 = jnp.concatenate([x[:, half:], -x[:, :half]], axis=1)
    scale = 1.0 / (time_count * spec_dev)
    o_ref[0, 0] = lax.dot_general(x, x, nt, preferred_element_type=jnp.float32) * scale
    o_ref[0, 1] = lax.dot_general(x2, x, nt, preferred_element_type=jnp.float32) * scale


def correlate(received, time_count, chan_count, capacity, inp_dev):
    width = received.shape[2]
    spec_dev = width // inp_dev
    inputs = chan_count * inp_dev
    kernel = functools.partial(correlate_kernel, time_count=time_count, inp_dev=inp_dev, caps=capacity)
    return pl.pallas_call(
        kernel,
        grid=(capacity,),
        in_specs=[pl.BlockSpec(received.shape, lambda c: (0, 0, 0))],
        out_specs=pl.BlockSpec((1, 2, inputs, inputs), lambda c: (c, 0, 0, 0)),
        out_shape=jax.ShapeDtypeStruct((capacity, 2, inputs, inputs), jnp.float32),
        scratch_shapes=[pltpu.VMEM((2 * time_count * spec_dev, inputs), jnp.float32)],
    )(received)


def solution(mesh):
    return jax.shard_map(
        local,
        mesh=mesh,
        in_specs=(P("chan", "tm", None, None), P(), P(), P()),
        out_specs=P(("chan", "tm"), None, None, None),
        check_vma=False,
    )
```

```python
import functools
import math

import jax
import jax.numpy as jnp
from jax import lax
from jax.experimental import pallas as pl
from jax.experimental.pallas import tpu as pltpu
from jax.sharding import PartitionSpec as P


def from_behind(value, axis, by):
    count = lax.axis_size(axis)
    pairs = [(i, i + by) for i in range(count) if 0 <= i + by < count]
    return lax.ppermute(value, axis, pairs)


def slot_table(flagged, owners, channels, devices):
    channel_ids = jnp.arange(channels, dtype=jnp.int32)
    alive_mask = jnp.ones((channels,), jnp.bool_).at[flagged].set(False)
    count = jnp.zeros((devices,), jnp.int32).at[owners].add(alive_mask.astype(jnp.int32))
    lower = jnp.full((devices,), channels, jnp.int32).at[owners].min(jnp.where(alive_mask, channel_ids, channels))
    upper = jnp.zeros((devices,), jnp.int32).at[owners].max(jnp.where(alive_mask, channel_ids, 0))
    chosen = jnp.stack([jnp.where(count > 0, lower, 0), jnp.where(count > 1, upper, 0)], axis=1)
    present = jnp.stack([count > 0, count > 1], axis=1)
    return (chosen.reshape(-1), present.reshape(-1))


def slot_tables(chosen, present, channels):
    low = 32
    high = channels // low
    step = 2.0 * math.pi / channels
    hi = jnp.arange(high, dtype=jnp.int32)
    lo = jnp.arange(low, dtype=jnp.int32)
    angle_hi = ((hi[:, None] * low * chosen[None, :]) % channels).astype(jnp.float32) * step
    angle_lo = ((lo[:, None] * chosen[None, :]) % channels).astype(jnp.float32) * step
    factor = 1.0 / math.sqrt(channels)
    keep = jnp.where(present, factor, 0.0).astype(jnp.float32)[None, :]
    c1, s1 = jnp.cos(angle_hi)[:, None, :], jnp.sin(angle_hi)[:, None, :]
    c2, s2 = (jnp.cos(angle_lo) * keep)[None, :, :], (jnp.sin(angle_lo) * keep)[None, :, :]
    cos_rows = (c1 * c2 - s1 * s2).reshape(channels, -1)
    sin_rows = (s1 * c2 + c1 * s2).reshape(channels, -1)
    return cos_rows.astype(jnp.bfloat16), sin_rows.astype(jnp.bfloat16)


def dft_kernel(x_ref, c0_ref, c1_ref, s0_ref, s1_ref, o_ref):
    x = x_ref[...]
    half = x.shape[0] // 2
    for cap, (c_ref, s_ref) in enumerate(((c0_ref, s0_ref), (c1_ref, s1_ref))):
        cos_part = jnp.dot(x, c_ref[...], preferred_element_type=jnp.float32)
        sin_part = jnp.dot(x, s_ref[...], preferred_element_type=jnp.float32)
        real_part = cos_part[:half] + sin_part[half:]
        imag_part = cos_part[half:] - sin_part[:half]
        o_ref[:, 2 * cap, :] = real_part.T.astype(o_ref.dtype)
        o_ref[:, 2 * cap + 1, :] = imag_part.T.astype(o_ref.dtype)


def dft_payload(filtered, cos_rows, sin_rows, devices, capacity):
    channels = filtered.shape[1]
    rows = filtered.shape[0] // 2
    block = 512
    steps = devices // block
    table_spec = lambda cap: pl.BlockSpec((channels, block), lambda j: (0, j + cap * steps))
    return pl.pallas_call(
        dft_kernel,
        grid=(steps,),
        in_specs=[
            pl.BlockSpec((2 * rows, channels), lambda j: (0, 0)),
            table_spec(0),
            table_spec(1),
            table_spec(0),
            table_spec(1),
        ],
        out_specs=pl.BlockSpec((block, capacity * 2, rows), lambda j: (j, 0, 0)),
        out_shape=jax.ShapeDtypeStruct((devices, capacity * 2, rows), jnp.bfloat16),
    )(filtered, cos_rows, cos_rows, sin_rows, sin_rows)


def local(voltages, filter_taps, flagged, owners):
    inp_dev = voltages.shape[0]
    spec_dev = voltages.shape[1]
    channels = voltages.shape[3]
    halo_depth = filter_taps.shape[0] - 1
    tail_block = voltages[:, spec_dev - halo_depth :]
    before = from_behind(tail_block, "tm", 1)
    joined = jnp.concatenate([before, voltages], axis=1).transpose(2, 0, 1, 3)
    running = jnp.zeros((2, inp_dev, spec_dev, channels), jnp.float32)
    for tap_index in range(halo_depth + 1):
        start_row = halo_depth - tap_index
        running = running + filter_taps[tap_index][None, None, None, :] * joined[
            :, :, start_row : start_row + spec_dev
        ].astype(jnp.float32)
    filtered = running.astype(jnp.bfloat16).reshape(2 * inp_dev * spec_dev, channels)

    chan_count = lax.axis_size("chan")
    time_count = lax.axis_size("tm")
    devices = chan_count * time_count
    capacity = channels // devices
    chosen, present = slot_table(flagged, owners, channels, devices)
    chosen = chosen.reshape(chan_count, time_count, capacity).transpose(2, 1, 0).reshape(-1)
    present = present.reshape(chan_count, time_count, capacity).transpose(2, 1, 0).reshape(-1)
    cos_rows, sin_rows = slot_tables(chosen, present, channels)
    sending = dft_payload(filtered, cos_rows, sin_rows, devices, capacity)
    received = lax.all_to_all(sending, ("tm", "chan"), 0, 0, tiled=True)
    return correlate(received, time_count, chan_count, capacity, inp_dev)


def correlate_kernel(r_ref, o_ref, xt_ref, *, time_count, inp_dev, caps):
    for cap in range(caps):
        pl.when(pl.program_id(0) == cap)(
            functools.partial(correlate_slot, r_ref, o_ref, xt_ref, cap, time_count, inp_dev)
        )


def correlate_slot(r_ref, o_ref, xt_ref, cap, time_count, inp_dev):
    chans = r_ref.shape[0] // time_count
    spec_dev = r_ref.shape[2] // inp_dev
    for reim in range(2):
        for tm in range(time_count):
            piece = r_ref[pl.ds(tm * chans, chans), cap * 2 + reim, :]
            block = piece.astype(jnp.float32).T
            row = (reim * time_count + tm) * spec_dev
            for i in range(inp_dev):
                xt_ref[row : row + spec_dev, i * chans : (i + 1) * chans] = block[
                    i * spec_dev : (i + 1) * spec_dev
                ]
    inputs = inp_dev * chans
    rows = lax.broadcasted_iota(jnp.int32, (inputs, inputs), 0)
    cols = lax.broadcasted_iota(jnp.int32, (inputs, inputs), 1)
    perm = (cols == (rows % inp_dev) * chans + rows // inp_dev).astype(jnp.bfloat16)
    nt = (((1,), (1,)), ((), ()))
    xt = xt_ref[...].astype(jnp.bfloat16)
    x = lax.dot_general(perm, xt, nt, preferred_element_type=jnp.float32).astype(jnp.bfloat16)
    half = x.shape[1] // 2
    x2 = jnp.concatenate([x[:, half:], -x[:, :half]], axis=1)
    scale = 1.0 / (time_count * spec_dev)
    o_ref[0, 0] = lax.dot_general(x, x, nt, preferred_element_type=jnp.float32) * scale
    o_ref[0, 1] = lax.dot_general(x2, x, nt, preferred_element_type=jnp.float32) * scale


def correlate(received, time_count, chan_count, capacity, inp_dev):
    width = received.shape[2]
    spec_dev = width // inp_dev
    inputs = chan_count * inp_dev
    kernel = functools.partial(correlate_kernel, time_count=time_count, inp_dev=inp_dev, caps=capacity)
    return pl.pallas_call(
        kernel,
        grid=(capacity,),
        in_specs=[pl.BlockSpec(received.shape, lambda c: (0, 0, 0))],
        out_specs=pl.BlockSpec((1, 2, inputs, inputs), lambda c: (c, 0, 0, 0)),
        out_shape=jax.ShapeDtypeStruct((capacity, 2, inputs, inputs), jnp.float32),
        scratch_shapes=[pltpu.VMEM((2 * time_count * spec_dev, inputs), jnp.float32)],
    )(received)


def solution(mesh):
    return jax.shard_map(
        local,
        mesh=mesh,
        in_specs=(P("chan", "tm", None, None), P(), P(), P()),
        out_specs=P(("chan", "tm"), None, None, None),
        check_vma=False,
    )
```

```python
import functools
import math

import jax
import jax.numpy as jnp
from jax import lax
from jax.experimental import pallas as pl
from jax.experimental.pallas import tpu as pltpu
from jax.sharding import PartitionSpec as P


def from_behind(value, axis, by):
    count = lax.axis_size(axis)
    pairs = [(i, i + by) for i in range(count) if 0 <= i + by < count]
    return lax.ppermute(value, axis, pairs)


def slot_table(flagged, owners, channels, devices):
    channel_ids = jnp.arange(channels, dtype=jnp.int32)
    alive_mask = jnp.logical_not(jnp.any(flagged[:, None] == channel_ids[None, :], axis=0))
    device_ids = jnp.arange(devices, dtype=jnp.int32)
    mine = (owners[:, None] == device_ids[None, :]) & alive_mask[:, None]
    count = jnp.sum(mine.astype(jnp.int32), axis=0)
    lower = jnp.min(jnp.where(mine, channel_ids[:, None], channels), axis=0)
    upper = jnp.max(jnp.where(mine, channel_ids[:, None], 0), axis=0)
    chosen = jnp.stack([jnp.where(count > 0, lower, 0), jnp.where(count > 1, upper, 0)], axis=1)
    present = jnp.stack([count > 0, count > 1], axis=1)
    return (chosen.reshape(-1), present.reshape(-1))


def slot_tables(chosen, present, channels):
    low = 32
    high = channels // low
    step = 2.0 * math.pi / channels
    hi = jnp.arange(high, dtype=jnp.int32)
    lo = jnp.arange(low, dtype=jnp.int32)
    angle_hi = ((hi[:, None] * low * chosen[None, :]) % channels).astype(jnp.float32) * step
    angle_lo = ((lo[:, None] * chosen[None, :]) % channels).astype(jnp.float32) * step
    c1, s1 = jnp.cos(angle_hi)[:, None, :], jnp.sin(angle_hi)[:, None, :]
    c2, s2 = jnp.cos(angle_lo)[None, :, :], jnp.sin(angle_lo)[None, :, :]
    factor = 1.0 / math.sqrt(channels)
    keep = jnp.where(present, factor, 0.0).astype(jnp.float32)[None, None, :]
    cos_rows = ((c1 * c2 - s1 * s2) * keep).reshape(channels, -1)
    sin_rows = ((s1 * c2 + c1 * s2) * keep).reshape(channels, -1)
    return cos_rows.astype(jnp.bfloat16), sin_rows.astype(jnp.bfloat16)


def dft_kernel(x_ref, c0_ref, c1_ref, s0_ref, s1_ref, o_ref):
    x = x_ref[...]
    half = x.shape[0] // 2
    for cap, (c_ref, s_ref) in enumerate(((c0_ref, s0_ref), (c1_ref, s1_ref))):
        cos_part = jnp.dot(x, c_ref[...], preferred_element_type=jnp.float32)
        sin_part = jnp.dot(x, s_ref[...], preferred_element_type=jnp.float32)
        real_part = cos_part[:half] + sin_part[half:]
        imag_part = cos_part[half:] - sin_part[:half]
        o_ref[:, 2 * cap, :] = real_part.T.astype(o_ref.dtype)
        o_ref[:, 2 * cap + 1, :] = imag_part.T.astype(o_ref.dtype)


def dft_payload(filtered, cos_rows, sin_rows, devices, capacity):
    channels = filtered.shape[1]
    rows = filtered.shape[0] // 2
    block = 512
    steps = devices // block
    table_spec = lambda cap: pl.BlockSpec((channels, block), lambda j: (0, j + cap * steps))
    return pl.pallas_call(
        dft_kernel,
        grid=(steps,),
        in_specs=[
            pl.BlockSpec((2 * rows, channels), lambda j: (0, 0)),
            table_spec(0),
            table_spec(1),
            table_spec(0),
            table_spec(1),
        ],
        out_specs=pl.BlockSpec((block, capacity * 2, rows), lambda j: (j, 0, 0)),
        out_shape=jax.ShapeDtypeStruct((devices, capacity * 2, rows), jnp.bfloat16),
    )(filtered, cos_rows, cos_rows, sin_rows, sin_rows)


def local(voltages, filter_taps, flagged, owners):
    inp_dev = voltages.shape[0]
    spec_dev = voltages.shape[1]
    channels = voltages.shape[3]
    halo_depth = filter_taps.shape[0] - 1
    tail_block = voltages[:, spec_dev - halo_depth :]
    before = from_behind(tail_block, "tm", 1)
    joined = jnp.concatenate([before, voltages], axis=1).transpose(2, 0, 1, 3)
    running = jnp.zeros((2, inp_dev, spec_dev, channels), jnp.float32)
    for tap_index in range(halo_depth + 1):
        start_row = halo_depth - tap_index
        running = running + filter_taps[tap_index][None, None, None, :] * joined[
            :, :, start_row : start_row + spec_dev
        ].astype(jnp.float32)
    filtered = running.astype(jnp.bfloat16).reshape(2 * inp_dev * spec_dev, channels)

    chan_count = lax.axis_size("chan")
    time_count = lax.axis_size("tm")
    devices = chan_count * time_count
    capacity = channels // devices
    chosen, present = slot_table(flagged, owners, channels, devices)
    chosen = chosen.reshape(chan_count, time_count, capacity).transpose(2, 1, 0).reshape(-1)
    present = present.reshape(chan_count, time_count, capacity).transpose(2, 1, 0).reshape(-1)
    cos_rows, sin_rows = slot_tables(chosen, present, channels)
    sending = dft_payload(filtered, cos_rows, sin_rows, devices, capacity)
    received = lax.all_to_all(sending, ("tm", "chan"), 0, 0, tiled=True)
    return correlate(received, time_count, chan_count, capacity, inp_dev)


def correlate_kernel(r_ref, o_ref, xt_ref, *, time_count, inp_dev, caps):
    for cap in range(caps):
        pl.when(pl.program_id(0) == cap)(
            functools.partial(correlate_slot, r_ref, o_ref, xt_ref, cap, time_count, inp_dev)
        )


def correlate_slot(r_ref, o_ref, xt_ref, cap, time_count, inp_dev):
    chans = r_ref.shape[0] // time_count
    spec_dev = r_ref.shape[2] // inp_dev
    for reim in range(2):
        for tm in range(time_count):
            piece = r_ref[pl.ds(tm * chans, chans), cap * 2 + reim, :]
            block = piece.astype(jnp.float32).T
            row = (reim * time_count + tm) * spec_dev
            for i in range(inp_dev):
                xt_ref[row : row + spec_dev, i * chans : (i + 1) * chans] = block[
                    i * spec_dev : (i + 1) * spec_dev
                ]
    inputs = inp_dev * chans
    rows = lax.broadcasted_iota(jnp.int32, (inputs, inputs), 0)
    cols = lax.broadcasted_iota(jnp.int32, (inputs, inputs), 1)
    perm = (cols == (rows % inp_dev) * chans + rows // inp_dev).astype(jnp.bfloat16)
    nt = (((1,), (1,)), ((), ()))
    xt = xt_ref[...].astype(jnp.bfloat16)
    x = lax.dot_general(perm, xt, nt, preferred_element_type=jnp.float32).astype(jnp.bfloat16)
    half = x.shape[1] // 2
    x2 = jnp.concatenate([x[:, half:], -x[:, :half]], axis=1)
    scale = 1.0 / (time_count * spec_dev)
    o_ref[0, 0] = lax.dot_general(x, x, nt, preferred_element_type=jnp.float32) * scale
    o_ref[0, 1] = lax.dot_general(x2, x, nt, preferred_element_type=jnp.float32) * scale


def correlate(received, time_count, chan_count, capacity, inp_dev):
    width = received.shape[2]
    spec_dev = width // inp_dev
    inputs = chan_count * inp_dev
    kernel = functools.partial(correlate_kernel, time_count=time_count, inp_dev=inp_dev, caps=capacity)
    return pl.pallas_call(
        kernel,
        grid=(capacity,),
        in_specs=[pl.BlockSpec(received.shape, lambda c: (0, 0, 0))],
        out_specs=pl.BlockSpec((1, 2, inputs, inputs), lambda c: (c, 0, 0, 0)),
        out_shape=jax.ShapeDtypeStruct((capacity, 2, inputs, inputs), jnp.float32),
        scratch_shapes=[pltpu.VMEM((2 * time_count * spec_dev, inputs), jnp.float32)],
    )(received)


def solution(mesh):
    return jax.shard_map(
        local,
        mesh=mesh,
        in_specs=(P("chan", "tm", None, None), P(), P(), P()),
        out_specs=P(("chan", "tm"), None, None, None),
        check_vma=False,
    )
```

```python
import functools
import math

import jax
import jax.numpy as jnp
from jax import lax
from jax.experimental import pallas as pl
from jax.experimental.pallas import tpu as pltpu
from jax.sharding import PartitionSpec as P


def from_behind(value, axis, by):
    count = lax.axis_size(axis)
    pairs = [(i, i + by) for i in range(count) if 0 <= i + by < count]
    return lax.ppermute(value, axis, pairs)


def slot_table(flagged, owners, channels, devices):
    channel_ids = jnp.arange(channels, dtype=jnp.int32)
    alive_mask = jnp.logical_not(jnp.any(flagged[:, None] == channel_ids[None, :], axis=0))
    device_ids = jnp.arange(devices, dtype=jnp.int32)
    mine = (owners[:, None] == device_ids[None, :]) & alive_mask[:, None]
    count = jnp.sum(mine.astype(jnp.int32), axis=0)
    lower = jnp.min(jnp.where(mine, channel_ids[:, None], channels), axis=0)
    upper = jnp.max(jnp.where(mine, channel_ids[:, None], 0), axis=0)
    chosen = jnp.stack([jnp.where(count > 0, lower, 0), jnp.where(count > 1, upper, 0)], axis=1)
    present = jnp.stack([count > 0, count > 1], axis=1)
    return (chosen.reshape(-1), present.reshape(-1))


def slot_tables(chosen, present, channels):
    low = 32
    high = channels // low
    step = 2.0 * math.pi / channels
    hi = jnp.arange(high, dtype=jnp.int32)
    lo = jnp.arange(low, dtype=jnp.int32)
    angle_hi = ((hi[:, None] * low * chosen[None, :]) % channels).astype(jnp.float32) * step
    angle_lo = ((lo[:, None] * chosen[None, :]) % channels).astype(jnp.float32) * step
    c1, s1 = jnp.cos(angle_hi)[:, None, :], jnp.sin(angle_hi)[:, None, :]
    c2, s2 = jnp.cos(angle_lo)[None, :, :], jnp.sin(angle_lo)[None, :, :]
    factor = 1.0 / math.sqrt(channels)
    keep = jnp.where(present, factor, 0.0).astype(jnp.float32)[None, None, :]
    cos_rows = ((c1 * c2 - s1 * s2) * keep).reshape(channels, -1)
    sin_rows = ((s1 * c2 + c1 * s2) * keep).reshape(channels, -1)
    return cos_rows.astype(jnp.bfloat16), sin_rows.astype(jnp.bfloat16)


def dft_kernel(x_ref, c0_ref, c1_ref, s0_ref, s1_ref, o_ref):
    x = x_ref[...]
    half = x.shape[0] // 2
    tn = (((0,), (1,)), ((), ()))
    for cap, (c_ref, s_ref) in enumerate(((c0_ref, s0_ref), (c1_ref, s1_ref))):
        cos_part = lax.dot_general(c_ref[...], x, tn, preferred_element_type=jnp.float32)
        sin_part = lax.dot_general(s_ref[...], x, tn, preferred_element_type=jnp.float32)
        o_ref[:, 2 * cap, :] = (cos_part[:, :half] + sin_part[:, half:]).astype(o_ref.dtype)
        o_ref[:, 2 * cap + 1, :] = (cos_part[:, half:] - sin_part[:, :half]).astype(o_ref.dtype)


def dft_payload(filtered, cos_rows, sin_rows, devices, capacity):
    channels = filtered.shape[1]
    rows = filtered.shape[0] // 2
    block = 512
    steps = devices // block
    table_spec = lambda cap: pl.BlockSpec((channels, block), lambda j: (0, j + cap * steps))
    return pl.pallas_call(
        dft_kernel,
        grid=(steps,),
        in_specs=[
            pl.BlockSpec((2 * rows, channels), lambda j: (0, 0)),
            table_spec(0),
            table_spec(1),
            table_spec(0),
            table_spec(1),
        ],
        out_specs=pl.BlockSpec((block, capacity * 2, rows), lambda j: (j, 0, 0)),
        out_shape=jax.ShapeDtypeStruct((devices, capacity * 2, rows), jnp.bfloat16),
    )(filtered, cos_rows, cos_rows, sin_rows, sin_rows)


def local(voltages, filter_taps, flagged, owners):
    inp_dev = voltages.shape[0]
    spec_dev = voltages.shape[1]
    channels = voltages.shape[3]
    halo_depth = filter_taps.shape[0] - 1
    tail_block = voltages[:, spec_dev - halo_depth :]
    before = from_behind(tail_block, "tm", 1)
    joined = jnp.concatenate([before, voltages], axis=1).transpose(2, 0, 1, 3)
    running = jnp.zeros((2, inp_dev, spec_dev, channels), jnp.float32)
    for tap_index in range(halo_depth + 1):
        start_row = halo_depth - tap_index
        running = running + filter_taps[tap_index][None, None, None, :] * joined[
            :, :, start_row : start_row + spec_dev
        ].astype(jnp.float32)
    filtered = running.astype(jnp.bfloat16).reshape(2 * inp_dev * spec_dev, channels)

    chan_count = lax.axis_size("chan")
    time_count = lax.axis_size("tm")
    devices = chan_count * time_count
    capacity = channels // devices
    chosen, present = slot_table(flagged, owners, channels, devices)
    chosen = chosen.reshape(chan_count, time_count, capacity).transpose(2, 1, 0).reshape(-1)
    present = present.reshape(chan_count, time_count, capacity).transpose(2, 1, 0).reshape(-1)
    cos_rows, sin_rows = slot_tables(chosen, present, channels)
    sending = dft_payload(filtered, cos_rows, sin_rows, devices, capacity)
    received = lax.all_to_all(sending, ("tm", "chan"), 0, 0, tiled=True)
    return correlate(received, time_count, chan_count, capacity, inp_dev)


def correlate_kernel(r_ref, o_ref, xt_ref, *, time_count, inp_dev, caps):
    for cap in range(caps):
        pl.when(pl.program_id(0) == cap)(
            functools.partial(correlate_slot, r_ref, o_ref, xt_ref, cap, time_count, inp_dev)
        )


def correlate_slot(r_ref, o_ref, xt_ref, cap, time_count, inp_dev):
    chans = r_ref.shape[0] // time_count
    spec_dev = r_ref.shape[2] // inp_dev
    for reim in range(2):
        for tm in range(time_count):
            piece = r_ref[pl.ds(tm * chans, chans), cap * 2 + reim, :]
            block = piece.astype(jnp.float32).T
            row = (reim * time_count + tm) * spec_dev
            for i in range(inp_dev):
                xt_ref[row : row + spec_dev, i * chans : (i + 1) * chans] = block[
                    i * spec_dev : (i + 1) * spec_dev
                ]
    inputs = inp_dev * chans
    rows = lax.broadcasted_iota(jnp.int32, (inputs, inputs), 0)
    cols = lax.broadcasted_iota(jnp.int32, (inputs, inputs), 1)
    perm = (cols == (rows % inp_dev) * chans + rows // inp_dev).astype(jnp.bfloat16)
    nt = (((1,), (1,)), ((), ()))
    xt = xt_ref[...].astype(jnp.bfloat16)
    x = lax.dot_general(perm, xt, nt, preferred_element_type=jnp.float32).astype(jnp.bfloat16)
    half = x.shape[1] // 2
    x2 = jnp.concatenate([x[:, half:], -x[:, :half]], axis=1)
    scale = 1.0 / (time_count * spec_dev)
    o_ref[0, 0] = lax.dot_general(x, x, nt, preferred_element_type=jnp.float32) * scale
    o_ref[0, 1] = lax.dot_general(x2, x, nt, preferred_element_type=jnp.float32) * scale


def correlate(received, time_count, chan_count, capacity, inp_dev):
    width = received.shape[2]
    spec_dev = width // inp_dev
    inputs = chan_count * inp_dev
    kernel = functools.partial(correlate_kernel, time_count=time_count, inp_dev=inp_dev, caps=capacity)
    return pl.pallas_call(
        kernel,
        grid=(capacity,),
        in_specs=[pl.BlockSpec(received.shape, lambda c: (0, 0, 0))],
        out_specs=pl.BlockSpec((1, 2, inputs, inputs), lambda c: (c, 0, 0, 0)),
        out_shape=jax.ShapeDtypeStruct((capacity, 2, inputs, inputs), jnp.float32),
        scratch_shapes=[pltpu.VMEM((2 * time_count * spec_dev, inputs), jnp.float32)],
    )(received)


def solution(mesh):
    return jax.shard_map(
        local,
        mesh=mesh,
        in_specs=(P("chan", "tm", None, None), P(), P(), P()),
        out_specs=P(("chan", "tm"), None, None, None),
        check_vma=False,
    )
```

```python
import functools
import math

import jax
import jax.numpy as jnp
from jax import lax
from jax.experimental import pallas as pl
from jax.experimental.pallas import tpu as pltpu
from jax.sharding import PartitionSpec as P


def from_behind(value, axis, by):
    count = lax.axis_size(axis)
    pairs = [(i, i + by) for i in range(count) if 0 <= i + by < count]
    return lax.ppermute(value, axis, pairs)


def slot_table(flagged, owners, channels, devices):
    channel_ids = jnp.arange(channels, dtype=jnp.int32)
    alive_mask = jnp.logical_not(jnp.any(flagged[:, None] == channel_ids[None, :], axis=0))
    device_ids = jnp.arange(devices, dtype=jnp.int32)
    mine = (owners[:, None] == device_ids[None, :]) & alive_mask[:, None]
    count = jnp.sum(mine.astype(jnp.int32), axis=0)
    lower = jnp.min(jnp.where(mine, channel_ids[:, None], channels), axis=0)
    upper = jnp.max(jnp.where(mine, channel_ids[:, None], 0), axis=0)
    chosen = jnp.stack([jnp.where(count > 0, lower, 0), jnp.where(count > 1, upper, 0)], axis=1)
    present = jnp.stack([count > 0, count > 1], axis=1)
    return (chosen.reshape(-1), present.reshape(-1))


def slot_factors(chosen, present, channels):
    low = 32
    high = channels // low
    step = 2.0 * math.pi / channels
    hi = jnp.arange(high, dtype=jnp.int32)
    lo = jnp.arange(low, dtype=jnp.int32)
    angle_hi = ((hi[:, None] * low * chosen[None, :]) % channels).astype(jnp.float32) * step
    angle_lo = ((lo[:, None] * chosen[None, :]) % channels).astype(jnp.float32) * step
    keep = jnp.where(present, 1.0 / math.sqrt(channels), 0.0).astype(jnp.float32)[None, :]
    return (jnp.cos(angle_hi), jnp.sin(angle_hi), jnp.cos(angle_lo) * keep, jnp.sin(angle_lo) * keep)


def dft_kernel(x_ref, *refs):
    factor_refs, o_ref = refs[:-1], refs[-1]
    x = x_ref[...]
    half = x.shape[0] // 2
    channels = x.shape[1]
    tn = (((0,), (1,)), ((), ()))
    for cap in range(len(factor_refs) // 4):
        c1, s1, c2, s2 = (r[...] for r in factor_refs[4 * cap : 4 * cap + 4])
        c1, s1 = c1[:, None, :], s1[:, None, :]
        c2, s2 = c2[None, :, :], s2[None, :, :]
        cos_rows = (c1 * c2 - s1 * s2).reshape(channels, -1).astype(jnp.bfloat16)
        sin_rows = (s1 * c2 + c1 * s2).reshape(channels, -1).astype(jnp.bfloat16)
        cos_part = lax.dot_general(cos_rows, x, tn, preferred_element_type=jnp.float32)
        sin_part = lax.dot_general(sin_rows, x, tn, preferred_element_type=jnp.float32)
        o_ref[:, 2 * cap, :] = (cos_part[:, :half] + sin_part[:, half:]).astype(o_ref.dtype)
        o_ref[:, 2 * cap + 1, :] = (cos_part[:, half:] - sin_part[:, :half]).astype(o_ref.dtype)


def dft_payload(filtered, factors, devices, capacity):
    channels = filtered.shape[1]
    rows = filtered.shape[0] // 2
    block = 512
    steps = devices // block
    specs = []
    operands = []
    for cap in range(capacity):
        for f in factors:
            specs.append(pl.BlockSpec((f.shape[0], block), lambda j, cap=cap: (0, j + cap * steps)))
            operands.append(f)
    return pl.pallas_call(
        dft_kernel,
        grid=(steps,),
        in_specs=[pl.BlockSpec((2 * rows, channels), lambda j: (0, 0))] + specs,
        out_specs=pl.BlockSpec((block, capacity * 2, rows), lambda j: (j, 0, 0)),
        out_shape=jax.ShapeDtypeStruct((devices, capacity * 2, rows), jnp.bfloat16),
    )(filtered, *operands)


def local(voltages, filter_taps, flagged, owners):
    inp_dev = voltages.shape[0]
    spec_dev = voltages.shape[1]
    channels = voltages.shape[3]
    halo_depth = filter_taps.shape[0] - 1
    tail_block = voltages[:, spec_dev - halo_depth :]
    before = from_behind(tail_block, "tm", 1)
    joined = jnp.concatenate([before, voltages], axis=1).transpose(2, 0, 1, 3)
    running = jnp.zeros((2, inp_dev, spec_dev, channels), jnp.float32)
    for tap_index in range(halo_depth + 1):
        start_row = halo_depth - tap_index
        running = running + filter_taps[tap_index][None, None, None, :] * joined[
            :, :, start_row : start_row + spec_dev
        ].astype(jnp.float32)
    filtered = running.astype(jnp.bfloat16).reshape(2 * inp_dev * spec_dev, channels)

    chan_count = lax.axis_size("chan")
    time_count = lax.axis_size("tm")
    devices = chan_count * time_count
    capacity = channels // devices
    chosen, present = slot_table(flagged, owners, channels, devices)
    chosen = chosen.reshape(chan_count, time_count, capacity).transpose(2, 1, 0).reshape(-1)
    present = present.reshape(chan_count, time_count, capacity).transpose(2, 1, 0).reshape(-1)
    factors = slot_factors(chosen, present, channels)
    sending = dft_payload(filtered, factors, devices, capacity)
    received = lax.all_to_all(sending, ("tm", "chan"), 0, 0, tiled=True)
    return correlate(received, time_count, chan_count, capacity, inp_dev)


def correlate_kernel(r_ref, o_ref, xt_ref, *, time_count, inp_dev, caps):
    for cap in range(caps):
        pl.when(pl.program_id(0) == cap)(
            functools.partial(correlate_slot, r_ref, o_ref, xt_ref, cap, time_count, inp_dev)
        )


def correlate_slot(r_ref, o_ref, xt_ref, cap, time_count, inp_dev):
    chans = r_ref.shape[0] // time_count
    spec_dev = r_ref.shape[2] // inp_dev
    for reim in range(2):
        for tm in range(time_count):
            piece = r_ref[pl.ds(tm * chans, chans), cap * 2 + reim, :]
            block = piece.astype(jnp.float32).T
            row = (reim * time_count + tm) * spec_dev
            for i in range(inp_dev):
                xt_ref[row : row + spec_dev, i * chans : (i + 1) * chans] = block[
                    i * spec_dev : (i + 1) * spec_dev
                ]
    inputs = inp_dev * chans
    rows = lax.broadcasted_iota(jnp.int32, (inputs, inputs), 0)
    cols = lax.broadcasted_iota(jnp.int32, (inputs, inputs), 1)
    perm = (cols == (rows % inp_dev) * chans + rows // inp_dev).astype(jnp.bfloat16)
    nt = (((1,), (1,)), ((), ()))
    xt = xt_ref[...].astype(jnp.bfloat16)
    x = lax.dot_general(perm, xt, nt, preferred_element_type=jnp.float32).astype(jnp.bfloat16)
    half = x.shape[1] // 2
    x2 = jnp.concatenate([x[:, half:], -x[:, :half]], axis=1)
    scale = 1.0 / (time_count * spec_dev)
    o_ref[0, 0] = lax.dot_general(x, x, nt, preferred_element_type=jnp.float32) * scale
    o_ref[0, 1] = lax.dot_general(x2, x, nt, preferred_element_type=jnp.float32) * scale


def correlate(received, time_count, chan_count, capacity, inp_dev):
    width = received.shape[2]
    spec_dev = width // inp_dev
    inputs = chan_count * inp_dev
    kernel = functools.partial(correlate_kernel, time_count=time_count, inp_dev=inp_dev, caps=capacity)
    return pl.pallas_call(
        kernel,
        grid=(capacity,),
        in_specs=[pl.BlockSpec(received.shape, lambda c: (0, 0, 0))],
        out_specs=pl.BlockSpec((1, 2, inputs, inputs), lambda c: (c, 0, 0, 0)),
        out_shape=jax.ShapeDtypeStruct((capacity, 2, inputs, inputs), jnp.float32),
        scratch_shapes=[pltpu.VMEM((2 * time_count * spec_dev, inputs), jnp.float32)],
    )(received)


def solution(mesh):
    return jax.shard_map(
        local,
        mesh=mesh,
        in_specs=(P("chan", "tm", None, None), P(), P(), P()),
        out_specs=P(("chan", "tm"), None, None, None),
        check_vma=False,
    )
```

```python
import functools
import math

import jax
import jax.numpy as jnp
from jax import lax
from jax.experimental import pallas as pl
from jax.experimental.pallas import tpu as pltpu
from jax.sharding import PartitionSpec as P


def from_behind(value, axis, by):
    count = lax.axis_size(axis)
    pairs = [(i, i + by) for i in range(count) if 0 <= i + by < count]
    return lax.ppermute(value, axis, pairs)


def slot_table(flagged, owners, channels, devices):
    channel_ids = jnp.arange(channels, dtype=jnp.int32)
    alive_mask = jnp.logical_not(jnp.any(flagged[:, None] == channel_ids[None, :], axis=0))
    device_ids = jnp.arange(devices, dtype=jnp.int32)
    mine = (owners[:, None] == device_ids[None, :]) & alive_mask[:, None]
    count = jnp.sum(mine.astype(jnp.int32), axis=0)
    lower = jnp.min(jnp.where(mine, channel_ids[:, None], channels), axis=0)
    upper = jnp.max(jnp.where(mine, channel_ids[:, None], 0), axis=0)
    chosen = jnp.stack([jnp.where(count > 0, lower, 0), jnp.where(count > 1, upper, 0)], axis=1)
    present = jnp.stack([count > 0, count > 1], axis=1)
    return (chosen.reshape(-1), present.reshape(-1))


def slot_factors(chosen, present, channels):
    low = 32
    high = channels // low
    step = 2.0 * math.pi / channels
    hi = jnp.arange(high, dtype=jnp.int32)
    lo = jnp.arange(low, dtype=jnp.int32)
    angle_hi = ((hi[:, None] * low * chosen[None, :]) % channels).astype(jnp.float32) * step
    angle_lo = ((lo[:, None] * chosen[None, :]) % channels).astype(jnp.float32) * step
    keep = jnp.where(present, 1.0 / math.sqrt(channels), 0.0).astype(jnp.float32)[None, :]
    return (jnp.cos(angle_hi), jnp.sin(angle_hi), jnp.cos(angle_lo) * keep, jnp.sin(angle_lo) * keep)


def dft_kernel(x_ref, *refs):
    factor_refs, o_ref = refs[:-1], refs[-1]
    x = x_ref[...]
    half = x.shape[0] // 2
    channels = x.shape[1]
    tn = (((0,), (1,)), ((), ()))
    for cap in range(len(factor_refs) // 4):
        c1, s1, c2, s2 = (r[...] for r in factor_refs[4 * cap : 4 * cap + 4])
        c1, s1 = c1[:, None, :], s1[:, None, :]
        c2, s2 = c2[None, :, :], s2[None, :, :]
        cos_rows = (c1 * c2 - s1 * s2).reshape(channels, -1).astype(jnp.bfloat16)
        sin_rows = (s1 * c2 + c1 * s2).reshape(channels, -1).astype(jnp.bfloat16)
        cos_part = lax.dot_general(cos_rows, x, tn, preferred_element_type=jnp.float32)
        sin_part = lax.dot_general(sin_rows, x, tn, preferred_element_type=jnp.float32)
        o_ref[:, 2 * cap, :] = (cos_part[:, :half] + sin_part[:, half:]).astype(o_ref.dtype)
        o_ref[:, 2 * cap + 1, :] = (cos_part[:, half:] - sin_part[:, :half]).astype(o_ref.dtype)


def dft_payload(filtered, factors, devices, capacity):
    channels = filtered.shape[1]
    rows = filtered.shape[0] // 2
    block = 512
    steps = devices // block
    specs = []
    operands = []
    for cap in range(capacity):
        for f in factors:
            specs.append(pl.BlockSpec((f.shape[0], block), lambda j, cap=cap: (0, j + cap * steps)))
            operands.append(f)
    return pl.pallas_call(
        dft_kernel,
        grid=(steps,),
        in_specs=[pl.BlockSpec((2 * rows, channels), lambda j: (0, 0))] + specs,
        out_specs=pl.BlockSpec((block, capacity * 2, rows), lambda j: (j, 0, 0)),
        out_shape=jax.ShapeDtypeStruct((devices, capacity * 2, rows), jnp.bfloat16),
    )(filtered, *operands)


def local(voltages, filter_taps, flagged, owners):
    inp_dev = voltages.shape[0]
    spec_dev = voltages.shape[1]
    channels = voltages.shape[3]
    halo_depth = filter_taps.shape[0] - 1
    tail_block = voltages[:, spec_dev - halo_depth :]
    before = from_behind(tail_block, "tm", 1)
    joined = jnp.concatenate([before, voltages], axis=1).transpose(2, 0, 1, 3)
    running = jnp.zeros((2, inp_dev, spec_dev, channels), jnp.float32)
    for tap_index in range(halo_depth + 1):
        start_row = halo_depth - tap_index
        running = running + filter_taps[tap_index][None, None, None, :] * joined[
            :, :, start_row : start_row + spec_dev
        ].astype(jnp.float32)
    filtered = running.astype(jnp.bfloat16).reshape(2 * inp_dev * spec_dev, channels)

    chan_count = lax.axis_size("chan")
    time_count = lax.axis_size("tm")
    devices = chan_count * time_count
    capacity = channels // devices
    chosen, present = slot_table(flagged, owners, channels, devices)
    chosen = chosen.reshape(chan_count, time_count, capacity).transpose(2, 1, 0).reshape(-1)
    present = present.reshape(chan_count, time_count, capacity).transpose(2, 1, 0).reshape(-1)
    factors = slot_factors(chosen, present, channels)
    sending = dft_payload(filtered, factors, devices, capacity)
    received = lax.all_to_all(sending, ("tm", "chan"), 0, 0, tiled=True)
    return correlate(received, time_count, chan_count, capacity, inp_dev)


def correlate_kernel(r_ref, o_ref, xt_ref, *, time_count, inp_dev, caps):
    for cap in range(caps):
        pl.when(pl.program_id(0) == cap)(
            functools.partial(correlate_slot, r_ref, o_ref, xt_ref, cap, time_count, inp_dev)
        )


def correlate_slot(r_ref, o_ref, xt_ref, cap, time_count, inp_dev):
    chans = r_ref.shape[0] // time_count
    spec_dev = r_ref.shape[2] // inp_dev
    for reim in range(2):
        for tm in range(time_count):
            piece = r_ref[pl.ds(tm * chans, chans), cap * 2 + reim, :]
            block = piece.T
            row = (reim * time_count + tm) * spec_dev
            for i in range(inp_dev):
                xt_ref[row : row + spec_dev, i * chans : (i + 1) * chans] = block[
                    i * spec_dev : (i + 1) * spec_dev
                ]
    inputs = inp_dev * chans
    rows = lax.broadcasted_iota(jnp.int32, (inputs, inputs), 0)
    cols = lax.broadcasted_iota(jnp.int32, (inputs, inputs), 1)
    perm = (cols == (rows % inp_dev) * chans + rows // inp_dev).astype(jnp.bfloat16)
    nt = (((1,), (1,)), ((), ()))
    xt = xt_ref[...]
    x = lax.dot_general(perm, xt, nt, preferred_element_type=jnp.float32).astype(jnp.bfloat16)
    half = x.shape[1] // 2
    x2 = jnp.concatenate([x[:, half:], -x[:, :half]], axis=1)
    scale = 1.0 / (time_count * spec_dev)
    o_ref[0, 0] = lax.dot_general(x, x, nt, preferred_element_type=jnp.float32) * scale
    o_ref[0, 1] = lax.dot_general(x2, x, nt, preferred_element_type=jnp.float32) * scale


def correlate(received, time_count, chan_count, capacity, inp_dev):
    width = received.shape[2]
    spec_dev = width // inp_dev
    inputs = chan_count * inp_dev
    kernel = functools.partial(correlate_kernel, time_count=time_count, inp_dev=inp_dev, caps=capacity)
    return pl.pallas_call(
        kernel,
        grid=(capacity,),
        in_specs=[pl.BlockSpec(received.shape, lambda c: (0, 0, 0))],
        out_specs=pl.BlockSpec((1, 2, inputs, inputs), lambda c: (c, 0, 0, 0)),
        out_shape=jax.ShapeDtypeStruct((capacity, 2, inputs, inputs), jnp.float32),
        scratch_shapes=[pltpu.VMEM((2 * time_count * spec_dev, inputs), jnp.bfloat16)],
    )(received)


def solution(mesh):
    return jax.shard_map(
        local,
        mesh=mesh,
        in_specs=(P("chan", "tm", None, None), P(), P(), P()),
        out_specs=P(("chan", "tm"), None, None, None),
        check_vma=False,
    )
```

```python
import functools
import math

import jax
import jax.numpy as jnp
from jax import lax
from jax.experimental import pallas as pl
from jax.experimental.pallas import tpu as pltpu
from jax.sharding import PartitionSpec as P


def from_behind(value, axis, by):
    count = lax.axis_size(axis)
    pairs = [(i, i + by) for i in range(count) if 0 <= i + by < count]
    return lax.ppermute(value, axis, pairs)


def slot_table(flagged, owners, channels, devices):
    channel_ids = jnp.arange(channels, dtype=jnp.int32)
    alive_mask = jnp.logical_not(jnp.any(flagged[:, None] == channel_ids[None, :], axis=0))
    device_ids = jnp.arange(devices, dtype=jnp.int32)
    mine = (owners[:, None] == device_ids[None, :]) & alive_mask[:, None]
    count = jnp.sum(mine.astype(jnp.int32), axis=0)
    lower = jnp.min(jnp.where(mine, channel_ids[:, None], channels), axis=0)
    upper = jnp.max(jnp.where(mine, channel_ids[:, None], 0), axis=0)
    chosen = jnp.stack([jnp.where(count > 0, lower, 0), jnp.where(count > 1, upper, 0)], axis=1)
    present = jnp.stack([count > 0, count > 1], axis=1)
    return (chosen.reshape(-1), present.reshape(-1))


def slot_factors(chosen, present, channels):
    low = 32
    high = channels // low
    step = 2.0 * math.pi / channels
    hi = jnp.arange(high, dtype=jnp.int32)
    lo = jnp.arange(low, dtype=jnp.int32)
    angle_hi = ((hi[:, None] * low * chosen[None, :]) % channels).astype(jnp.float32) * step
    angle_lo = ((lo[:, None] * chosen[None, :]) % channels).astype(jnp.float32) * step
    keep = jnp.where(present, 1.0 / math.sqrt(channels), 0.0).astype(jnp.float32)[None, :]
    return (jnp.cos(angle_hi), jnp.sin(angle_hi), jnp.cos(angle_lo) * keep, jnp.sin(angle_lo) * keep)


def dft_kernel(x_ref, *refs):
    factor_refs, o_ref = refs[:-1], refs[-1]
    x = x_ref[...]
    half = x.shape[0] // 2
    channels = x.shape[1]
    tn = (((0,), (1,)), ((), ()))
    for cap in range(len(factor_refs) // 4):
        c1, s1, c2, s2 = (r[...] for r in factor_refs[4 * cap : 4 * cap + 4])
        c1, s1 = c1[:, None, :], s1[:, None, :]
        c2, s2 = c2[None, :, :], s2[None, :, :]
        cos_rows = (c1 * c2 - s1 * s2).reshape(channels, -1).astype(jnp.bfloat16)
        sin_rows = (s1 * c2 + c1 * s2).reshape(channels, -1).astype(jnp.bfloat16)
        cos_part = lax.dot_general(cos_rows, x, tn, preferred_element_type=jnp.float32)
        sin_part = lax.dot_general(sin_rows, x, tn, preferred_element_type=jnp.float32)
        o_ref[:, 2 * cap, :] = (cos_part[:, :half] + sin_part[:, half:]).astype(o_ref.dtype)
        o_ref[:, 2 * cap + 1, :] = (cos_part[:, half:] - sin_part[:, :half]).astype(o_ref.dtype)


def dft_payload(filtered, factors, devices, capacity):
    channels = filtered.shape[1]
    rows = filtered.shape[0] // 2
    block = 256
    steps = devices // block
    specs = []
    operands = []
    for cap in range(capacity):
        for f in factors:
            specs.append(pl.BlockSpec((f.shape[0], block), lambda j, cap=cap: (0, j + cap * steps)))
            operands.append(f)
    return pl.pallas_call(
        dft_kernel,
        grid=(steps,),
        in_specs=[pl.BlockSpec((2 * rows, channels), lambda j: (0, 0))] + specs,
        out_specs=pl.BlockSpec((block, capacity * 2, rows), lambda j: (j, 0, 0)),
        out_shape=jax.ShapeDtypeStruct((devices, capacity * 2, rows), jnp.bfloat16),
    )(filtered, *operands)


def local(voltages, filter_taps, flagged, owners):
    inp_dev = voltages.shape[0]
    spec_dev = voltages.shape[1]
    channels = voltages.shape[3]
    halo_depth = filter_taps.shape[0] - 1
    tail_block = voltages[:, spec_dev - halo_depth :]
    before = from_behind(tail_block, "tm", 1)
    joined = jnp.concatenate([before, voltages], axis=1).transpose(2, 0, 1, 3)
    running = jnp.zeros((2, inp_dev, spec_dev, channels), jnp.float32)
    for tap_index in range(halo_depth + 1):
        start_row = halo_depth - tap_index
        running = running + filter_taps[tap_index][None, None, None, :] * joined[
            :, :, start_row : start_row + spec_dev
        ].astype(jnp.float32)
    filtered = running.astype(jnp.bfloat16).reshape(2 * inp_dev * spec_dev, channels)

    chan_count = lax.axis_size("chan")
    time_count = lax.axis_size("tm")
    devices = chan_count * time_count
    capacity = channels // devices
    chosen, present = slot_table(flagged, owners, channels, devices)
    chosen = chosen.reshape(chan_count, time_count, capacity).transpose(2, 1, 0).reshape(-1)
    present = present.reshape(chan_count, time_count, capacity).transpose(2, 1, 0).reshape(-1)
    factors = slot_factors(chosen, present, channels)
    sending = dft_payload(filtered, factors, devices, capacity)
    received = lax.all_to_all(sending, ("tm", "chan"), 0, 0, tiled=True)
    return correlate(received, time_count, chan_count, capacity, inp_dev)


def correlate_kernel(r_ref, o_ref, xt_ref, *, time_count, inp_dev, caps):
    for cap in range(caps):
        pl.when(pl.program_id(0) == cap)(
            functools.partial(correlate_slot, r_ref, o_ref, xt_ref, cap, time_count, inp_dev)
        )


def correlate_slot(r_ref, o_ref, xt_ref, cap, time_count, inp_dev):
    chans = r_ref.shape[0] // time_count
    spec_dev = r_ref.shape[2] // inp_dev
    for reim in range(2):
        for tm in range(time_count):
            piece = r_ref[pl.ds(tm * chans, chans), cap * 2 + reim, :]
            block = piece.astype(jnp.float32).T
            row = (reim * time_count + tm) * spec_dev
            for i in range(inp_dev):
                xt_ref[row : row + spec_dev, i * chans : (i + 1) * chans] = block[
                    i * spec_dev : (i + 1) * spec_dev
                ]
    inputs = inp_dev * chans
    rows = lax.broadcasted_iota(jnp.int32, (inputs, inputs), 0)
    cols = lax.broadcasted_iota(jnp.int32, (inputs, inputs), 1)
    perm = (cols == (rows % inp_dev) * chans + rows // inp_dev).astype(jnp.bfloat16)
    nt = (((1,), (1,)), ((), ()))
    xt = xt_ref[...].astype(jnp.bfloat16)
    x = lax.dot_general(perm, xt, nt, preferred_element_type=jnp.float32).astype(jnp.bfloat16)
    half = x.shape[1] // 2
    x2 = jnp.concatenate([x[:, half:], -x[:, :half]], axis=1)
    scale = 1.0 / (time_count * spec_dev)
    o_ref[0, 0] = lax.dot_general(x, x, nt, preferred_element_type=jnp.float32) * scale
    o_ref[0, 1] = lax.dot_general(x2, x, nt, preferred_element_type=jnp.float32) * scale


def correlate(received, time_count, chan_count, capacity, inp_dev):
    width = received.shape[2]
    spec_dev = width // inp_dev
    inputs = chan_count * inp_dev
    kernel = functools.partial(correlate_kernel, time_count=time_count, inp_dev=inp_dev, caps=capacity)
    return pl.pallas_call(
        kernel,
        grid=(capacity,),
        in_specs=[pl.BlockSpec(received.shape, lambda c: (0, 0, 0))],
        out_specs=pl.BlockSpec((1, 2, inputs, inputs), lambda c: (c, 0, 0, 0)),
        out_shape=jax.ShapeDtypeStruct((capacity, 2, inputs, inputs), jnp.float32),
        scratch_shapes=[pltpu.VMEM((2 * time_count * spec_dev, inputs), jnp.float32)],
    )(received)


def solution(mesh):
    return jax.shard_map(
        local,
        mesh=mesh,
        in_specs=(P("chan", "tm", None, None), P(), P(), P()),
        out_specs=P(("chan", "tm"), None, None, None),
        check_vma=False,
    )
```

```python
import functools
import math

import jax
import jax.numpy as jnp
from jax import lax
from jax.experimental import pallas as pl
from jax.experimental.pallas import tpu as pltpu
from jax.sharding import PartitionSpec as P


def from_behind(value, axis, by):
    count = lax.axis_size(axis)
    pairs = [(i, i + by) for i in range(count) if 0 <= i + by < count]
    return lax.ppermute(value, axis, pairs)


def slot_table(flagged, owners, channels, devices):
    channel_ids = jnp.arange(channels, dtype=jnp.int32)
    alive_mask = jnp.logical_not(jnp.any(flagged[:, None] == channel_ids[None, :], axis=0))
    device_ids = jnp.arange(devices, dtype=jnp.int32)
    mine = (owners[:, None] == device_ids[None, :]) & alive_mask[:, None]
    count = jnp.sum(mine.astype(jnp.int32), axis=0)
    lower = jnp.min(jnp.where(mine, channel_ids[:, None], channels), axis=0)
    upper = jnp.max(jnp.where(mine, channel_ids[:, None], 0), axis=0)
    chosen = jnp.stack([jnp.where(count > 0, lower, 0), jnp.where(count > 1, upper, 0)], axis=1)
    present = jnp.stack([count > 0, count > 1], axis=1)
    return (chosen.reshape(-1), present.reshape(-1))


def slot_factors(chosen, present, channels):
    low = 32
    high = channels // low
    step = 2.0 * math.pi / channels
    top = jnp.arange(high // 4, dtype=jnp.int32)
    rest = jnp.arange(4, dtype=jnp.int32)
    lo = jnp.arange(low, dtype=jnp.int32)
    angle_top = ((top[:, None] * (4 * low) * chosen[None, :]) % channels).astype(jnp.float32) * step
    angle_rest = ((rest[:, None] * low * chosen[None, :]) % channels).astype(jnp.float32) * step
    angle_lo = ((lo[:, None] * chosen[None, :]) % channels).astype(jnp.float32) * step
    ct, st = jnp.cos(angle_top)[:, None, :], jnp.sin(angle_top)[:, None, :]
    cr, sr = jnp.cos(angle_rest)[None, :, :], jnp.sin(angle_rest)[None, :, :]
    cos_hi = (ct * cr - st * sr).reshape(high, -1)
    sin_hi = (st * cr + ct * sr).reshape(high, -1)
    keep = jnp.where(present, 1.0 / math.sqrt(channels), 0.0).astype(jnp.float32)[None, :]
    return (cos_hi, sin_hi, jnp.cos(angle_lo) * keep, jnp.sin(angle_lo) * keep)


def dft_kernel(x_ref, *refs):
    factor_refs, o_ref = refs[:-1], refs[-1]
    x = x_ref[...]
    half = x.shape[0] // 2
    channels = x.shape[1]
    tn = (((0,), (1,)), ((), ()))
    for cap in range(len(factor_refs) // 4):
        c1, s1, c2, s2 = (r[...] for r in factor_refs[4 * cap : 4 * cap + 4])
        c1, s1 = c1[:, None, :], s1[:, None, :]
        c2, s2 = c2[None, :, :], s2[None, :, :]
        cos_rows = (c1 * c2 - s1 * s2).reshape(channels, -1).astype(jnp.bfloat16)
        sin_rows = (s1 * c2 + c1 * s2).reshape(channels, -1).astype(jnp.bfloat16)
        cos_part = lax.dot_general(cos_rows, x, tn, preferred_element_type=jnp.float32)
        sin_part = lax.dot_general(sin_rows, x, tn, preferred_element_type=jnp.float32)
        o_ref[:, 2 * cap, :] = (cos_part[:, :half] + sin_part[:, half:]).astype(o_ref.dtype)
        o_ref[:, 2 * cap + 1, :] = (cos_part[:, half:] - sin_part[:, :half]).astype(o_ref.dtype)


def dft_payload(filtered, factors, devices, capacity):
    channels = filtered.shape[1]
    rows = filtered.shape[0] // 2
    block = 512
    steps = devices // block
    specs = []
    operands = []
    for cap in range(capacity):
        for f in factors:
            specs.append(pl.BlockSpec((f.shape[0], block), lambda j, cap=cap: (0, j + cap * steps)))
            operands.append(f)
    return pl.pallas_call(
        dft_kernel,
        grid=(steps,),
        in_specs=[pl.BlockSpec((2 * rows, channels), lambda j: (0, 0))] + specs,
        out_specs=pl.BlockSpec((block, capacity * 2, rows), lambda j: (j, 0, 0)),
        out_shape=jax.ShapeDtypeStruct((devices, capacity * 2, rows), jnp.bfloat16),
    )(filtered, *operands)


def local(voltages, filter_taps, flagged, owners):
    inp_dev = voltages.shape[0]
    spec_dev = voltages.shape[1]
    channels = voltages.shape[3]
    halo_depth = filter_taps.shape[0] - 1
    tail_block = voltages[:, spec_dev - halo_depth :]
    before = from_behind(tail_block, "tm", 1)
    joined = jnp.concatenate([before, voltages], axis=1).transpose(2, 0, 1, 3)
    running = jnp.zeros((2, inp_dev, spec_dev, channels), jnp.float32)
    for tap_index in range(halo_depth + 1):
        start_row = halo_depth - tap_index
        running = running + filter_taps[tap_index][None, None, None, :] * joined[
            :, :, start_row : start_row + spec_dev
        ].astype(jnp.float32)
    filtered = running.astype(jnp.bfloat16).reshape(2 * inp_dev * spec_dev, channels)

    chan_count = lax.axis_size("chan")
    time_count = lax.axis_size("tm")
    devices = chan_count * time_count
    capacity = channels // devices
    chosen, present = slot_table(flagged, owners, channels, devices)
    chosen = chosen.reshape(chan_count, time_count, capacity).transpose(2, 1, 0).reshape(-1)
    present = present.reshape(chan_count, time_count, capacity).transpose(2, 1, 0).reshape(-1)
    factors = slot_factors(chosen, present, channels)
    sending = dft_payload(filtered, factors, devices, capacity)
    received = lax.all_to_all(sending, ("tm", "chan"), 0, 0, tiled=True)
    return correlate(received, time_count, chan_count, capacity, inp_dev)


def correlate_kernel(r_ref, o_ref, xt_ref, *, time_count, inp_dev, caps):
    for cap in range(caps):
        pl.when(pl.program_id(0) == cap)(
            functools.partial(correlate_slot, r_ref, o_ref, xt_ref, cap, time_count, inp_dev)
        )


def correlate_slot(r_ref, o_ref, xt_ref, cap, time_count, inp_dev):
    chans = r_ref.shape[0] // time_count
    spec_dev = r_ref.shape[2] // inp_dev
    for reim in range(2):
        for tm in range(time_count):
            piece = r_ref[pl.ds(tm * chans, chans), cap * 2 + reim, :]
            block = piece.astype(jnp.float32).T
            row = (reim * time_count + tm) * spec_dev
            for i in range(inp_dev):
                xt_ref[row : row + spec_dev, i * chans : (i + 1) * chans] = block[
                    i * spec_dev : (i + 1) * spec_dev
                ]
    inputs = inp_dev * chans
    rows = lax.broadcasted_iota(jnp.int32, (inputs, inputs), 0)
    cols = lax.broadcasted_iota(jnp.int32, (inputs, inputs), 1)
    perm = (cols == (rows % inp_dev) * chans + rows // inp_dev).astype(jnp.bfloat16)
    nt = (((1,), (1,)), ((), ()))
    xt = xt_ref[...].astype(jnp.bfloat16)
    x = lax.dot_general(perm, xt, nt, preferred_element_type=jnp.float32).astype(jnp.bfloat16)
    half = x.shape[1] // 2
    x2 = jnp.concatenate([x[:, half:], -x[:, :half]], axis=1)
    scale = 1.0 / (time_count * spec_dev)
    o_ref[0, 0] = lax.dot_general(x, x, nt, preferred_element_type=jnp.float32) * scale
    o_ref[0, 1] = lax.dot_general(x2, x, nt, preferred_element_type=jnp.float32) * scale


def correlate(received, time_count, chan_count, capacity, inp_dev):
    width = received.shape[2]
    spec_dev = width // inp_dev
    inputs = chan_count * inp_dev
    kernel = functools.partial(correlate_kernel, time_count=time_count, inp_dev=inp_dev, caps=capacity)
    return pl.pallas_call(
        kernel,
        grid=(capacity,),
        in_specs=[pl.BlockSpec(received.shape, lambda c: (0, 0, 0))],
        out_specs=pl.BlockSpec((1, 2, inputs, inputs), lambda c: (c, 0, 0, 0)),
        out_shape=jax.ShapeDtypeStruct((capacity, 2, inputs, inputs), jnp.float32),
        scratch_shapes=[pltpu.VMEM((2 * time_count * spec_dev, inputs), jnp.float32)],
    )(received)


def solution(mesh):
    return jax.shard_map(
        local,
        mesh=mesh,
        in_specs=(P("chan", "tm", None, None), P(), P(), P()),
        out_specs=P(("chan", "tm"), None, None, None),
        check_vma=False,
    )
```

```python
import functools
import math

import jax
import jax.numpy as jnp
from jax import lax
from jax.experimental import pallas as pl
from jax.experimental.pallas import tpu as pltpu
from jax.sharding import PartitionSpec as P


def from_behind(value, axis, by):
    count = lax.axis_size(axis)
    pairs = [(i, i + by) for i in range(count) if 0 <= i + by < count]
    return lax.ppermute(value, axis, pairs)


def slot_table(flagged, owners, channels, devices):
    channel_ids = jnp.arange(channels, dtype=jnp.int32)
    alive_mask = jnp.logical_not(jnp.any(flagged[:, None] == channel_ids[None, :], axis=0))
    device_ids = jnp.arange(devices, dtype=jnp.int32)
    mine = (owners[:, None] == device_ids[None, :]) & alive_mask[:, None]
    count = jnp.sum(mine.astype(jnp.int32), axis=0)
    lower = jnp.min(jnp.where(mine, channel_ids[:, None], channels), axis=0)
    upper = jnp.max(jnp.where(mine, channel_ids[:, None], 0), axis=0)
    chosen = jnp.stack([jnp.where(count > 0, lower, 0), jnp.where(count > 1, upper, 0)], axis=1)
    present = jnp.stack([count > 0, count > 1], axis=1)
    return (chosen.reshape(-1), present.reshape(-1))


def slot_factors(chosen, present, channels):
    low = 32
    high = channels // low
    step = 2.0 * math.pi / channels
    hi = jnp.arange(high, dtype=jnp.int32)
    lo = jnp.arange(low, dtype=jnp.int32)
    angle_hi = ((hi[:, None] * low * chosen[None, :]) % channels).astype(jnp.float32) * step
    angle_lo = ((lo[:, None] * chosen[None, :]) % channels).astype(jnp.float32) * step
    keep = jnp.where(present, 1.0 / math.sqrt(channels), 0.0).astype(jnp.float32)[None, :]
    return (jnp.cos(angle_hi), jnp.sin(angle_hi), jnp.cos(angle_lo) * keep, jnp.sin(angle_lo) * keep)


def dft_kernel(x_ref, *refs):
    factor_refs, o_ref = refs[:-1], refs[-1]
    x = x_ref[...]
    half = x.shape[0] // 2
    channels = x.shape[1]
    tn = (((0,), (1,)), ((), ()))
    for cap in range(len(factor_refs) // 4):
        c1, s1, c2, s2 = (r[...] for r in factor_refs[4 * cap : 4 * cap + 4])
        c1, s1 = c1[:, None, :], s1[:, None, :]
        c2, s2 = c2[None, :, :], s2[None, :, :]
        cos_rows = (c1 * c2 - s1 * s2).reshape(channels, -1).astype(jnp.bfloat16)
        sin_rows = (s1 * c2 + c1 * s2).reshape(channels, -1).astype(jnp.bfloat16)
        cos_part = lax.dot_general(cos_rows, x, tn, preferred_element_type=jnp.float32)
        sin_part = lax.dot_general(sin_rows, x, tn, preferred_element_type=jnp.float32)
        o_ref[:, 2 * cap, :] = (cos_part[:, :half] + sin_part[:, half:]).astype(o_ref.dtype)
        o_ref[:, 2 * cap + 1, :] = (cos_part[:, half:] - sin_part[:, :half]).astype(o_ref.dtype)


def dft_payload(filtered, factors, devices, capacity):
    channels = filtered.shape[1]
    rows = filtered.shape[0] // 2
    block = 512
    steps = devices // block
    specs = []
    operands = []
    for cap in range(capacity):
        for f in factors:
            specs.append(pl.BlockSpec((f.shape[0], block), lambda j, cap=cap: (0, j + cap * steps)))
            operands.append(f)
    return pl.pallas_call(
        dft_kernel,
        grid=(steps,),
        in_specs=[pl.BlockSpec((2 * rows, channels), lambda j: (0, 0))] + specs,
        out_specs=pl.BlockSpec((block, capacity * 2, rows), lambda j: (j, 0, 0)),
        out_shape=jax.ShapeDtypeStruct((devices, capacity * 2, rows), jnp.bfloat16),
    )(filtered, *operands)


def local(voltages, filter_taps, flagged, owners):
    inp_dev = voltages.shape[0]
    spec_dev = voltages.shape[1]
    channels = voltages.shape[3]
    halo_depth = filter_taps.shape[0] - 1
    tail_block = voltages[:, spec_dev - halo_depth :]
    before = from_behind(tail_block, "tm", 1)
    joined = jnp.concatenate([before, voltages], axis=1).transpose(2, 0, 1, 3)
    running = jnp.zeros((2, inp_dev, spec_dev, channels), jnp.float32)
    for tap_index in range(halo_depth + 1):
        start_row = halo_depth - tap_index
        running = running + filter_taps[tap_index][None, None, None, :] * joined[
            :, :, start_row : start_row + spec_dev
        ].astype(jnp.float32)
    filtered = running.astype(jnp.bfloat16).reshape(2 * inp_dev * spec_dev, channels)

    chan_count = lax.axis_size("chan")
    time_count = lax.axis_size("tm")
    devices = chan_count * time_count
    capacity = channels // devices
    chosen, present = slot_table(flagged, owners, channels, devices)
    chosen = chosen.reshape(chan_count, time_count, capacity).transpose(2, 1, 0).reshape(-1)
    present = present.reshape(chan_count, time_count, capacity).transpose(2, 1, 0).reshape(-1)
    factors = slot_factors(chosen, present, channels)
    sending = dft_payload(filtered, factors, devices, capacity)
    received = lax.all_to_all(sending, ("tm", "chan"), 0, 0, tiled=True)
    return correlate(received, time_count, chan_count, capacity, inp_dev)


def correlate_kernel(r_ref, o_ref, xt_ref, *, time_count, inp_dev, caps):
    for cap in range(caps):
        correlate_slot(r_ref, o_ref.at[cap : cap + 1], xt_ref, cap, time_count, inp_dev)


def correlate_slot(r_ref, o_ref, xt_ref, cap, time_count, inp_dev):
    chans = r_ref.shape[0] // time_count
    spec_dev = r_ref.shape[2] // inp_dev
    for reim in range(2):
        for tm in range(time_count):
            piece = r_ref[pl.ds(tm * chans, chans), cap * 2 + reim, :]
            block = piece.astype(jnp.float32).T
            row = (reim * time_count + tm) * spec_dev
            for i in range(inp_dev):
                xt_ref[row : row + spec_dev, i * chans : (i + 1) * chans] = block[
                    i * spec_dev : (i + 1) * spec_dev
                ]
    inputs = inp_dev * chans
    rows = lax.broadcasted_iota(jnp.int32, (inputs, inputs), 0)
    cols = lax.broadcasted_iota(jnp.int32, (inputs, inputs), 1)
    perm = (cols == (rows % inp_dev) * chans + rows // inp_dev).astype(jnp.bfloat16)
    nt = (((1,), (1,)), ((), ()))
    xt = xt_ref[...].astype(jnp.bfloat16)
    x = lax.dot_general(perm, xt, nt, preferred_element_type=jnp.float32).astype(jnp.bfloat16)
    half = x.shape[1] // 2
    x2 = jnp.concatenate([x[:, half:], -x[:, :half]], axis=1)
    scale = 1.0 / (time_count * spec_dev)
    o_ref[0, 0] = lax.dot_general(x, x, nt, preferred_element_type=jnp.float32) * scale
    o_ref[0, 1] = lax.dot_general(x2, x, nt, preferred_element_type=jnp.float32) * scale


def correlate(received, time_count, chan_count, capacity, inp_dev):
    width = received.shape[2]
    spec_dev = width // inp_dev
    inputs = chan_count * inp_dev
    kernel = functools.partial(correlate_kernel, time_count=time_count, inp_dev=inp_dev, caps=capacity)
    return pl.pallas_call(
        kernel,
        grid=(1,),
        in_specs=[pl.BlockSpec(received.shape, lambda c: (0, 0, 0))],
        out_specs=pl.BlockSpec((capacity, 2, inputs, inputs), lambda c: (0, 0, 0, 0)),
        out_shape=jax.ShapeDtypeStruct((capacity, 2, inputs, inputs), jnp.float32),
        scratch_shapes=[pltpu.VMEM((2 * time_count * spec_dev, inputs), jnp.float32)],
    )(received)


def solution(mesh):
    return jax.shard_map(
        local,
        mesh=mesh,
        in_specs=(P("chan", "tm", None, None), P(), P(), P()),
        out_specs=P(("chan", "tm"), None, None, None),
        check_vma=False,
    )
```

```python
import functools
import math

import jax
import jax.numpy as jnp
from jax import lax
from jax.experimental import pallas as pl
from jax.experimental.pallas import tpu as pltpu
from jax.sharding import PartitionSpec as P


def from_behind(value, axis, by):
    count = lax.axis_size(axis)
    pairs = [(i, i + by) for i in range(count) if 0 <= i + by < count]
    return lax.ppermute(value, axis, pairs)


def slot_table(flagged, owners, channels, devices):
    channel_ids = jnp.arange(channels, dtype=jnp.int32)
    alive_mask = jnp.logical_not(jnp.any(flagged[:, None] == channel_ids[None, :], axis=0))
    device_ids = jnp.arange(devices, dtype=jnp.int32)
    mine = (owners[:, None] == device_ids[None, :]) & alive_mask[:, None]
    count = jnp.sum(mine.astype(jnp.int32), axis=0)
    lower = jnp.min(jnp.where(mine, channel_ids[:, None], channels), axis=0)
    upper = jnp.max(jnp.where(mine, channel_ids[:, None], 0), axis=0)
    chosen = jnp.stack([jnp.where(count > 0, lower, 0), jnp.where(count > 1, upper, 0)], axis=1)
    present = jnp.stack([count > 0, count > 1], axis=1)
    return (chosen.reshape(-1), present.reshape(-1))


def slot_factors(chosen, present, channels):
    low = 32
    high = channels // low
    step = 2.0 * math.pi / channels
    hi = jnp.arange(high, dtype=jnp.int32)
    lo = jnp.arange(low, dtype=jnp.int32)
    angle_hi = ((hi[:, None] * low * chosen[None, :]) % channels).astype(jnp.float32) * step
    angle_lo = ((lo[:, None] * chosen[None, :]) % channels).astype(jnp.float32) * step
    keep = jnp.where(present, 1.0 / math.sqrt(channels), 0.0).astype(jnp.float32)[None, :]
    return (jnp.cos(angle_hi), jnp.sin(angle_hi), jnp.cos(angle_lo) * keep, jnp.sin(angle_lo) * keep)


def dft_kernel(x_ref, *refs):
    factor_refs, o_ref = refs[:-1], refs[-1]
    x = x_ref[...]
    half = x.shape[0] // 2
    channels = x.shape[1]
    tn = (((0,), (1,)), ((), ()))
    for cap in range(len(factor_refs) // 4):
        c1, s1, c2, s2 = (r[...] for r in factor_refs[4 * cap : 4 * cap + 4])
        c1, s1 = c1[:, None, :], s1[:, None, :]
        c2, s2 = c2[None, :, :], s2[None, :, :]
        cos_rows = (c1 * c2 - s1 * s2).reshape(channels, -1).astype(jnp.bfloat16)
        sin_rows = (s1 * c2 + c1 * s2).reshape(channels, -1).astype(jnp.bfloat16)
        cos_part = lax.dot_general(cos_rows, x, tn, preferred_element_type=jnp.float32)
        sin_part = lax.dot_general(sin_rows, x, tn, preferred_element_type=jnp.float32)
        o_ref[:, 2 * cap, :] = (cos_part[:, :half] + sin_part[:, half:]).astype(o_ref.dtype)
        o_ref[:, 2 * cap + 1, :] = (cos_part[:, half:] - sin_part[:, :half]).astype(o_ref.dtype)


def dft_payload(filtered, factors, devices, capacity):
    channels = filtered.shape[1]
    rows = filtered.shape[0] // 2
    block = 512
    steps = devices // block
    specs = []
    operands = []
    for cap in range(capacity):
        for f in factors:
            specs.append(pl.BlockSpec((f.shape[0], block), lambda j, cap=cap: (0, j + cap * steps)))
            operands.append(f)
    return pl.pallas_call(
        dft_kernel,
        grid=(steps,),
        in_specs=[pl.BlockSpec((2 * rows, channels), lambda j: (0, 0))] + specs,
        out_specs=pl.BlockSpec((block, capacity * 2, rows), lambda j: (j, 0, 0)),
        out_shape=jax.ShapeDtypeStruct((devices, capacity * 2, rows), jnp.bfloat16),
    )(filtered, *operands)


def local(voltages, filter_taps, flagged, owners):
    inp_dev = voltages.shape[0]
    spec_dev = voltages.shape[1]
    channels = voltages.shape[3]
    halo_depth = filter_taps.shape[0] - 1
    tail_block = voltages[:, spec_dev - halo_depth :]
    before = from_behind(tail_block, "tm", 1)
    joined = jnp.concatenate([before, voltages], axis=1).transpose(2, 0, 1, 3)
    running = jnp.zeros((2, inp_dev, spec_dev, channels), jnp.float32)
    for tap_index in range(halo_depth + 1):
        start_row = halo_depth - tap_index
        running = running + filter_taps[tap_index][None, None, None, :] * joined[
            :, :, start_row : start_row + spec_dev
        ].astype(jnp.float32)
    filtered = running.astype(jnp.bfloat16).reshape(2 * inp_dev * spec_dev, channels)

    chan_count = lax.axis_size("chan")
    time_count = lax.axis_size("tm")
    devices = chan_count * time_count
    capacity = channels // devices
    chosen, present = slot_table(flagged, owners, channels, devices)
    chosen = chosen.reshape(chan_count, time_count, capacity).transpose(2, 1, 0).reshape(-1)
    present = present.reshape(chan_count, time_count, capacity).transpose(2, 1, 0).reshape(-1)
    factors = slot_factors(chosen, present, channels)
    sending = dft_payload(filtered, factors, devices, capacity)
    received = lax.all_to_all(sending, ("tm", "chan"), 0, 0, tiled=True)
    return correlate(received, time_count, chan_count, capacity, inp_dev)


def correlate_kernel(r_ref, o_ref, xt_ref, *, time_count, inp_dev, caps):
    for cap in range(caps):
        pl.when(pl.program_id(0) == cap)(
            functools.partial(correlate_slot, r_ref, o_ref, xt_ref, cap, time_count, inp_dev)
        )


def correlate_slot(r_ref, o_ref, xt_ref, cap, time_count, inp_dev):
    chans = r_ref.shape[0] // time_count
    spec_dev = r_ref.shape[2] // inp_dev
    for reim in range(2):
        for tm in range(time_count):
            piece = r_ref[pl.ds(tm * chans, chans), cap * 2 + reim, :]
            block = piece.astype(jnp.float32).T
            row = (reim * time_count + tm) * spec_dev
            for i in range(inp_dev):
                xt_ref[row : row + spec_dev, i * chans : (i + 1) * chans] = block[
                    i * spec_dev : (i + 1) * spec_dev
                ]
    inputs = inp_dev * chans
    rows = lax.broadcasted_iota(jnp.int32, (inputs, inputs), 0)
    cols = lax.broadcasted_iota(jnp.int32, (inputs, inputs), 1)
    perm = (cols == (rows % inp_dev) * chans + rows // inp_dev).astype(jnp.bfloat16)
    nt = (((1,), (1,)), ((), ()))
    xt = xt_ref[...].astype(jnp.bfloat16)
    x = lax.dot_general(perm, xt, nt, preferred_element_type=jnp.float32).astype(jnp.bfloat16)
    half = x.shape[1] // 2
    x2 = jnp.concatenate([x[:, half:], -x[:, :half]], axis=1)
    scale = jnp.asarray(1.0 / (time_count * spec_dev), jnp.bfloat16)
    o_ref[0, 0] = lax.dot_general(x * scale, x, nt, preferred_element_type=jnp.float32)
    o_ref[0, 1] = lax.dot_general(x2 * scale, x, nt, preferred_element_type=jnp.float32)


def correlate(received, time_count, chan_count, capacity, inp_dev):
    width = received.shape[2]
    spec_dev = width // inp_dev
    inputs = chan_count * inp_dev
    kernel = functools.partial(correlate_kernel, time_count=time_count, inp_dev=inp_dev, caps=capacity)
    return pl.pallas_call(
        kernel,
        grid=(capacity,),
        in_specs=[pl.BlockSpec(received.shape, lambda c: (0, 0, 0))],
        out_specs=pl.BlockSpec((1, 2, inputs, inputs), lambda c: (c, 0, 0, 0)),
        out_shape=jax.ShapeDtypeStruct((capacity, 2, inputs, inputs), jnp.float32),
        scratch_shapes=[pltpu.VMEM((2 * time_count * spec_dev, inputs), jnp.float32)],
    )(received)


def solution(mesh):
    return jax.shard_map(
        local,
        mesh=mesh,
        in_specs=(P("chan", "tm", None, None), P(), P(), P()),
        out_specs=P(("chan", "tm"), None, None, None),
        check_vma=False,
    )
```
